128 devices in a mesh: view: 4 (over y), block: 32 (over z, x, core).
Axes of the slice: x: 4, y: 4, z: 4, core: 2. Of those that a mesh axis runs over, the one named last changes fastest.
Arguments:
- estimate: float32 [512, 128, 256], P('block'), may hold values from 0.3 to 3
- observed: float32 [4, 512, 2, 128, 256], P('view', 'block'), may hold values from 0.2 to 5
- route_dest: int32 [4, 512], P('view', 'block'), may hold values from -1 to 31, as said below
- route_pos: int32 [4, 512], P('view', 'block'), may hold values from -1 to 15, as said below
- view_span: int32 [8, 2], P('view'), may hold values from 0 to 256, as said below
- view_count: int32 [256], P('block'), may hold values from 4 to 8, as said below
- psf_taps: float32 [8, 3, 31], P('view'), may hold values from 0 to 2, as said below
- view_weight: float32 [8], P('view'), may hold values from 1 to 4
Outputs:
- restored: float32 [512, 128, 256], P('block')
The draws below stay inside these ranges and needn't reach their ends.
Inputs may be any that keep to these rules, and one draw needn't show every extreme that they name: `route_dest`: in each view group, every brick of one of its views that lies inside that view's sub-volume stands in exactly one slot of the group's devices, with its owner block and position (view of the group times 8 plus brick of the block); other slots hold -1. One device's slots send at most 1 bricks to one block, and some device sends 1 to some block. `route_pos`: position of the slot's brick as described for route_dest, -1 together with it. `view_span`: each sub-volume lies within the 256 bricks and holds at least 128 of them; the first view of each view group spans all of them. `view_count`: equals the number of views whose span holds the brick. `psf_taps`: each kernel is positive.
All inputs are finite; a program needn't handle non-finite values.
Results may differ from the reference program's by a relative error of at most 0.0003.
Values sent between devices are 32-bit elements; how exact they have to be, the bound alone decides.
No kernel may reach another device: no remote copies, remote signals or barrier semaphores. Data moves between devices by JAX's collectives and lax.ppermute only.
A program may use at most 128 MiB of HBM per device.

```python
import math
import jax
import jax.numpy as jnp
from jax import lax

VPG = 2
TAPS = 31
BX = 2
BPS = 8
ITERS = 2
NY = 128
NZ = 256
VIEWS = 8
BRICKS = 256
NX = 512
SLOTS = 16


def span_table(key):
    base = jax.random.fold_in(key, 7)
    groups = VIEWS // VPG
    lengths = jax.random.randint(jax.random.fold_in(base, 1), (groups, VPG - 1), BRICKS // 2, BRICKS + 1)
    starts = jax.random.randint(jax.random.fold_in(base, 2), (groups, VPG - 1), 0, BRICKS - lengths + 1)
    leading_full_block = jnp.zeros((groups, 1), jnp.int32)
    length_full = jnp.full((groups, 1), BRICKS, jnp.int32)
    firsts = jnp.concatenate([leading_full_block, starts.astype(jnp.int32)], axis=1)
    spans = jnp.concatenate([length_full, lengths.astype(jnp.int32)], axis=1)
    return jnp.stack([firsts, spans], axis=-1).reshape(VIEWS, 2).astype(jnp.int32)


def route_table(key):
    spans = span_table(key)
    groups = VIEWS // VPG
    blocks = BRICKS // BPS
    shifts = jax.random.randint(jax.random.fold_in(key, 21), (groups,), 0, blocks)
    perm_keys = jax.random.split(jax.random.fold_in(key, 22), groups * blocks)
    perms = jax.vmap(lambda single: jax.random.permutation(single, SLOTS))(perm_keys)
    perms = perms.reshape(groups, blocks, SLOTS).astype(jnp.int32)
    source = jnp.arange(blocks, dtype=jnp.int32)[None, :, None]
    dest = (source - perms - shifts.astype(jnp.int32)[:, None, None]) % blocks
    view = jnp.arange(groups, dtype=jnp.int32)[:, None, None] * VPG + perms // BPS
    brick = dest * BPS + perms % BPS
    span_first = spans[view, 0]
    span_length = spans[view, 1]
    inside = (brick >= span_first) & (brick < span_first + span_length)
    dest_out = jnp.where(inside, dest, -1).reshape(groups, blocks * SLOTS).astype(jnp.int32)
    pos_out = jnp.where(inside, perms, -1).reshape(groups, blocks * SLOTS).astype(jnp.int32)
    return (dest_out, pos_out)


def draw_route_dest(key, part):
    return route_table(key)[0]


def draw_route_pos(key, part):
    return route_table(key)[1]


def draw_view_span(key, part):
    return span_table(key)


def draw_view_count(key, part):
    spans = span_table(key)
    brick_index = jnp.arange(BRICKS, dtype=jnp.int32)
    inside = (brick_index[None, :] >= spans[:, 0:1]) & (brick_index[None, :] < spans[:, 0:1] + spans[:, 1:2])
    return jnp.sum(inside.astype(jnp.int32), axis=0).astype(jnp.int32)


def draw_psf_taps(key, part):
    base = jax.random.fold_in(key, 41)
    centred = jnp.arange(TAPS, dtype=jnp.float32) - float(TAPS // 2)
    across = jnp.exp(jax.random.uniform(jax.random.fold_in(base, 4), (VIEWS, 1), jnp.float32, jnp.log(3.0), jnp.log(6.0)))
    lateral = jnp.exp(jax.random.uniform(jax.random.fold_in(base, 1), (VIEWS, 1), jnp.float32, jnp.log(1.5), jnp.log(3.0)))
    axial = jnp.exp(jax.random.uniform(jax.random.fold_in(base, 2), (VIEWS, 1), jnp.float32, jnp.log(3.0), jnp.log(6.0)))
    jitter = jax.random.uniform(jax.random.fold_in(base, 3), (VIEWS, 3, TAPS), jnp.float32, -0.2, 0.2)
    sigma = jnp.concatenate([across, lateral, axial], axis=1)[:, :, None]
    peak = jnp.exp(-centred[None, None, :] ** 2 / (2.0 * sigma * sigma))
    pedestal = jnp.array([0.05, 0.0, 0.0], jnp.float32)[None, :, None]
    return (peak * jnp.exp(jitter) + pedestal).astype(jnp.float32)


def block_scale(stream_key, dims, cuts, smallest, top_value):
    loudness, own = 1.0, jax.random.fold_in(stream_key, 6)
    for position, blocks in cuts:
        heights = jnp.exp(jax.random.uniform(jax.random.fold_in(own, position), (blocks,), jnp.float32, smallest / len(cuts), top_value / len(cuts)))
        loudness = loudness * jnp.repeat(heights, dims[position] // blocks).reshape([-1 if axis == position else 1 for axis in range(len(dims))])
    return loudness


def setup_inputs(seed: int = 0) -> dict:
    splits = jax.random.split(jax.random.key(seed), 9)
    estimate = jnp.clip(jnp.exp(math.log(3.0) - 2.3025851 * jax.random.uniform(splits[0], (NX, NY, NZ), jnp.float32) ** block_scale(splits[0], (NX, NY, NZ), ((0, 32),), -0.2, 0.2)), 0.3, 3.0)
    observed = jnp.clip(jnp.exp(math.log(5.0) - 3.218876 * jax.random.uniform(splits[1], (VIEWS // VPG, BRICKS // BPS * SLOTS, BX, NY, NZ), jnp.float32) ** block_scale(splits[1], (VIEWS // VPG, BRICKS // BPS * SLOTS, BX, NY, NZ), ((0, 4), (1, 32)), -0.2, 0.2)), 0.2, 5.0)
    route_dest = draw_route_dest(jax.random.fold_in(splits[8], 71), 0)
    route_pos = draw_route_pos(jax.random.fold_in(splits[8], 71), 0)
    view_span = draw_view_span(jax.random.fold_in(splits[8], 71), 0)
    view_count = draw_view_count(jax.random.fold_in(splits[8], 71), 0)
    psf_taps = draw_psf_taps(jax.random.fold_in(splits[8], 71), 0)
    view_weight = jnp.clip(jnp.exp(math.log(4.0) - 1.3862944 * jax.random.uniform(splits[7], (VIEWS,), jnp.float32) ** block_scale(splits[7], (VIEWS,), ((0, 4),), -0.2, 0.2)), 1.0, 4.0)
    return dict(estimate=estimate, observed=observed, route_dest=route_dest, route_pos=route_pos, view_span=view_span, view_count=view_count, psf_taps=psf_taps, view_weight=view_weight)


def banded_blur_matrix(filter_tap_values, row_count, col_count, offset_base, orientation):
    tap_count = filter_tap_values.shape[-1]
    grid_shape = (row_count, col_count, tap_count)
    row_index = lax.broadcasted_iota(jnp.int32, grid_shape, 0)
    col_index = lax.broadcasted_iota(jnp.int32, grid_shape, 1)
    tap_index = lax.broadcasted_iota(jnp.int32, grid_shape, 2)
    selected_entries = (orientation * (row_index - col_index) + offset_base == tap_index).astype(jnp.float32)
    return jnp.einsum("ewq,gq->gew", selected_entries, filter_tap_values, precision=lax.Precision.HIGHEST)


def blur_x(current, filter_tap_values, reverse):
    reach = TAPS // 2
    padded = jnp.pad(current, ((reach, reach), (0, 0), (0, 0)))
    summed = jnp.zeros_like(current)
    for offset in range(TAPS):
        weight_index = TAPS - 1 - offset if reverse else offset
        summed = summed + filter_tap_values[weight_index] * padded[offset:offset + NX]
    return summed


def reference(estimate, observed, route_dest, route_pos, view_span, view_count, psf_taps, view_weight):
    highest = lax.Precision.HIGHEST
    reach = TAPS // 2
    point_spread_kernels = psf_taps / jnp.sum(psf_taps, axis=-1, keepdims=True)
    mat_y = banded_blur_matrix(point_spread_kernels[:, 1], NY, NY, reach, 1)
    mat_z = banded_blur_matrix(point_spread_kernels[:, 2], NZ, NZ, reach, 1)
    brick_index = jnp.arange(BRICKS, dtype=jnp.int32)
    span_first = view_span[:, 0:1]
    span_length = view_span[:, 1:2]
    inside = ((brick_index[None, :] >= span_first) & (brick_index[None, :] < span_first + span_length)).astype(jnp.float32)
    live_cells = jnp.repeat(inside, BX, axis=1)
    counts = jnp.repeat(view_count.astype(jnp.float32), BX)[:, None, None]
    groups = VIEWS // VPG

    def group_obs(group):
        dest_list = route_dest[group]
        pos_list = route_pos[group]
        target = jnp.where(dest_list >= 0, (pos_list // BPS) * BRICKS + dest_list * BPS + pos_list % BPS, VPG * BRICKS)
        placed = jnp.zeros((VPG * BRICKS, BX, NY, NZ), jnp.float32).at[target].set(observed[group], mode="drop")
        return placed.reshape(VPG, NX, NY, NZ)

    current = estimate
    for iteration in range(ITERS):
        def add_group(summed, group):
            obs_views = group_obs(group)
            for local in range(VPG):
                view = group * VPG + local
                tap_x = point_spread_kernels[view, 0]
                blurred = blur_x(current, tap_x, False)
                blurred = jnp.einsum("xyz,yq->xqz", blurred, mat_y[view], precision=highest)
                blurred = jnp.einsum("xyz,zq->xyq", blurred, mat_z[view], precision=highest)
                cell_mask = live_cells[view][:, None, None]
                ratios = cell_mask * (obs_views[local] / blurred) + (1.0 - cell_mask)
                back = jnp.einsum("xyz,qz->xyq", ratios, mat_z[view], precision=highest)
                back = jnp.einsum("xyz,qy->xqz", back, mat_y[view], precision=highest)
                corrected = blur_x(back, tap_x, True)
                summed = summed + cell_mask * view_weight[view] * jnp.log(corrected)
            return summed, None

        summed, unused = lax.scan(add_group, jnp.zeros_like(current), jnp.arange(groups, dtype=jnp.int32))
        current = current * jnp.exp(summed / counts)
    return current
```

```python
import jax
import jax.numpy as jnp
from jax import lax
from jax.sharding import PartitionSpec as P

ITERS = 2


def with_halo(cells, sides, width):
    for axis, dim in sides:
        count = lax.axis_size(axis)
        ends = count - 1
        head = lax.slice_in_dim(cells, 0, width, axis=dim)
        tail = lax.slice_in_dim(cells, cells.shape[dim] - width, cells.shape[dim], axis=dim)
        cells = jnp.concatenate(
            [
                lax.ppermute(tail, axis, [(i, (i + 1) % count) for i in range(ends)]),
                cells,
                lax.ppermute(head, axis, [((i + 1) % count, i) for i in range(ends)]),
            ],
            axis=dim,
        )
    return cells


def view_sum_update(partial, current, counts):
    count = lax.axis_size("view")
    me = lax.axis_index("view")
    rows = partial.shape[0] // count

    def piece(cells, index):
        return lax.dynamic_slice_in_dim(cells, index * rows, rows, axis=0)

    summed = piece(partial, me)
    for shift in range(1, count):
        sent = piece(partial, (me + shift) % count)
        summed = summed + lax.ppermute(
            sent, "view", [(i, (i + shift) % count) for i in range(count)]
        )
    updated = piece(current, me) * jnp.exp(summed / piece(counts, me))
    gathered = lax.dynamic_update_slice_in_dim(current, updated, me * rows, axis=0)
    for shift in range(1, count):
        arrived = lax.ppermute(
            updated, "view", [(i, (i + shift) % count) for i in range(count)]
        )
        gathered = lax.dynamic_update_slice_in_dim(
            gathered, arrived, ((me - shift) % count) * rows, axis=0
        )
    return gathered


def banded_blur_matrix(filter_tap_values, row_count, col_count, offset_base, orientation):
    tap_count = filter_tap_values.shape[-1]
    grid_shape = (row_count, col_count, tap_count)
    row_index = lax.broadcasted_iota(jnp.int32, grid_shape, 0)
    col_index = lax.broadcasted_iota(jnp.int32, grid_shape, 1)
    tap_index = lax.broadcasted_iota(jnp.int32, grid_shape, 2)
    selected_entries = (orientation * (row_index - col_index) + offset_base == tap_index).astype(
        jnp.float32
    )
    return jnp.einsum(
        "ewq,gq->gew", selected_entries, filter_tap_values, precision=lax.Precision.HIGHEST
    )


def on_device(
    estimate, observed, route_dest, route_pos, view_span, view_count, psf_taps, view_weight
):
    highest = lax.Precision.HIGHEST
    blocks = lax.axis_size("block")
    slot_count = observed.shape[1]
    planes = observed.shape[2]
    ny_cells = observed.shape[3]
    nz_cells = observed.shape[4]
    per_group = view_span.shape[0]
    per_block = view_count.shape[0]
    capacity = max(1, slot_count // blocks)
    block_x = per_block * planes
    reach = psf_taps.shape[-1] // 2
    sources = observed[0]
    dest_list = route_dest[0]
    pos_list = route_pos[0]
    slot_index = jnp.arange(slot_count, dtype=jnp.int32)
    earlier = (dest_list[:, None] == dest_list[None, :]) & (
        slot_index[None, :] < slot_index[:, None]
    )
    rank_in_dest = jnp.sum(earlier.astype(jnp.int32), axis=1)
    target = jnp.where(dest_list >= 0, dest_list * capacity + rank_in_dest, blocks * capacity)
    outgoing = (
        jnp.zeros((blocks * capacity, planes, ny_cells, nz_cells), jnp.float32)
        .at[target]
        .set(sources, mode="drop")
    )
    out_pos = (
        jnp.full((blocks * capacity,), -1.0, jnp.float32)
        .at[target]
        .set(pos_list.astype(jnp.float32), mode="drop")
    )
    arrived, arrived_pos = (
        lax.all_to_all(
            outgoing.reshape(blocks, capacity, planes, ny_cells, nz_cells),
            "block",
            split_axis=0,
            concat_axis=0,
            tiled=True,
        ),
        lax.all_to_all(
            out_pos.reshape(blocks, capacity), "block", split_axis=0, concat_axis=0, tiled=True
        ),
    )
    places = arrived_pos.reshape(-1).astype(jnp.int32)
    places = jnp.where(places >= 0, places, per_group * per_block)
    placed = (
        jnp.zeros((per_group * per_block, planes, ny_cells, nz_cells), jnp.float32)
        .at[places]
        .set(arrived.reshape(-1, planes, ny_cells, nz_cells), mode="drop")
    )
    obs_views = placed.reshape(per_group, block_x, ny_cells, nz_cells)
    brick_index = lax.axis_index("block") * per_block + jnp.arange(per_block, dtype=jnp.int32)
    span_first = view_span[:, 0:1]
    span_length = view_span[:, 1:2]
    inside = (
        (brick_index[None, :] >= span_first) & (brick_index[None, :] < span_first + span_length)
    ).astype(jnp.float32)
    live_cells = jnp.repeat(inside, planes, axis=1)[:, :, None, None]
    counts = jnp.repeat(view_count.astype(jnp.float32), planes)[:, None, None]
    point_spread_kernels = psf_taps / jnp.sum(psf_taps, axis=-1, keepdims=True)
    fwd_x = banded_blur_matrix(point_spread_kernels[:, 0], block_x + 2 * reach, block_x, 0, 1)
    adj_x = banded_blur_matrix(
        point_spread_kernels[:, 0], block_x + 2 * reach, block_x, 2 * reach, -1
    )
    mat_y = banded_blur_matrix(point_spread_kernels[:, 1], ny_cells, ny_cells, reach, 1)
    mat_z = banded_blur_matrix(point_spread_kernels[:, 2], nz_cells, nz_cells, reach, 1)
    weights = view_weight[:, None, None, None]
    current = estimate
    for iteration in range(ITERS):
        padded = with_halo(current, (("block", 0),), reach)
        along_x = jnp.einsum("wyz,vwx->vxyz", padded, fwd_x, precision=highest)
        lateral_y_pass = jnp.einsum("vxyz,vyq->vxqz", along_x, mat_y, precision=highest)
        blurred = jnp.einsum("vxyz,vzq->vxyq", lateral_y_pass, mat_z, precision=highest)
        ratios = live_cells * (obs_views / blurred) + (1.0 - live_cells)
        back_z = jnp.einsum("vxyz,vqz->vxyq", ratios, mat_z, precision=highest)
        back_y = jnp.einsum("vxyz,vqy->vxqz", back_z, mat_y, precision=highest)
        rimmed = with_halo(back_y, (("block", 1),), reach)
        corrected = jnp.einsum("vwyz,vwx->vxyz", rimmed, adj_x, precision=highest)
        partial_logarithm = jnp.sum(live_cells * weights * jnp.log(corrected), axis=0)
        current = view_sum_update(partial_logarithm, current, counts)
    return current


def solution(mesh):
    placed = (
        P("block", None, None),
        P("view", "block", None, None, None),
        P("view", "block"),
        P("view", "block"),
        P("view", None),
        P("block"),
        P("view", None, None),
        P("view"),
    )
    return jax.shard_map(
        on_device, mesh=mesh, in_specs=placed, out_specs=P("block", None, None), check_vma=False
    )
```

```python
import jax
import jax.numpy as jnp
from jax import lax
from jax.sharding import PartitionSpec as P

ITERS = 2


def with_halo(cells, sides, width):
    for axis, dim in sides:
        count = lax.axis_size(axis)
        ends = count - 1
        head = lax.slice_in_dim(cells, 0, width, axis=dim)
        tail = lax.slice_in_dim(cells, cells.shape[dim] - width, cells.shape[dim], axis=dim)
        cells = jnp.concatenate(
            [
                lax.ppermute(tail, axis, [(i, (i + 1) % count) for i in range(ends)]),
                cells,
                lax.ppermute(head, axis, [((i + 1) % count, i) for i in range(ends)]),
            ],
            axis=dim,
        )
    return cells


def view_sum_update(partial, current, counts):
    count = lax.axis_size("view")
    me = lax.axis_index("view")
    rows = partial.shape[0] // count

    def piece(cells, index):
        return lax.dynamic_slice_in_dim(cells, index * rows, rows, axis=0)

    summed = piece(partial, me)
    for shift in range(1, count):
        sent = piece(partial, (me + shift) % count)
        summed = summed + lax.ppermute(
            sent, "view", [(i, (i + shift) % count) for i in range(count)]
        )
    updated = piece(current, me) * jnp.exp(summed / piece(counts, me))
    gathered = lax.dynamic_update_slice_in_dim(current, updated, me * rows, axis=0)
    for shift in range(1, count):
        arrived = lax.ppermute(
            updated, "view", [(i, (i + shift) % count) for i in range(count)]
        )
        gathered = lax.dynamic_update_slice_in_dim(
            gathered, arrived, ((me - shift) % count) * rows, axis=0
        )
    return gathered


def banded_blur_matrix(filter_tap_values, row_count, col_count, offset_base, orientation):
    tap_count = filter_tap_values.shape[-1]
    grid_shape = (row_count, col_count, tap_count)
    row_index = lax.broadcasted_iota(jnp.int32, grid_shape, 0)
    col_index = lax.broadcasted_iota(jnp.int32, grid_shape, 1)
    tap_index = lax.broadcasted_iota(jnp.int32, grid_shape, 2)
    selected_entries = (orientation * (row_index - col_index) + offset_base == tap_index).astype(
        jnp.float32
    )
    return jnp.einsum(
        "ewq,gq->gew", selected_entries, filter_tap_values, precision=lax.Precision.HIGHEST
    )


def on_device(
    estimate, observed, route_dest, route_pos, view_span, view_count, psf_taps, view_weight
):
    highest = lax.Precision.HIGHEST
    blocks = lax.axis_size("block")
    slot_count = observed.shape[1]
    planes = observed.shape[2]
    ny_cells = observed.shape[3]
    nz_cells = observed.shape[4]
    per_group = view_span.shape[0]
    per_block = view_count.shape[0]
    capacity = max(1, slot_count // blocks)
    block_x = per_block * planes
    reach = psf_taps.shape[-1] // 2
    sources = observed[0]
    dest_list = route_dest[0]
    pos_list = route_pos[0]
    slot_index = jnp.arange(slot_count, dtype=jnp.int32)
    earlier = (dest_list[:, None] == dest_list[None, :]) & (
        slot_index[None, :] < slot_index[:, None]
    )
    rank_in_dest = jnp.sum(earlier.astype(jnp.int32), axis=1)
    target = jnp.where(dest_list >= 0, dest_list * capacity + rank_in_dest, blocks * capacity)
    outgoing = (
        jnp.zeros((blocks * capacity, planes, ny_cells, nz_cells), jnp.float32)
        .at[target]
        .set(sources, mode="drop")
    )
    out_pos = (
        jnp.full((blocks * capacity,), -1.0, jnp.float32)
        .at[target]
        .set(pos_list.astype(jnp.float32), mode="drop")
    )
    arrived, arrived_pos = (
        lax.all_to_all(
            outgoing.reshape(blocks, capacity, planes, ny_cells, nz_cells),
            "block",
            split_axis=0,
            concat_axis=0,
            tiled=True,
        ),
        lax.all_to_all(
            out_pos.reshape(blocks, capacity), "block", split_axis=0, concat_axis=0, tiled=True
        ),
    )
    places = arrived_pos.reshape(-1).astype(jnp.int32)
    places = jnp.where(places >= 0, places, per_group * per_block)
    placed = (
        jnp.zeros((per_group * per_block, planes, ny_cells, nz_cells), jnp.float32)
        .at[places]
        .set(arrived.reshape(-1, planes, ny_cells, nz_cells), mode="drop")
    )
    obs_views = placed.reshape(per_group, block_x, ny_cells, nz_cells)
    brick_index = lax.axis_index("block") * per_block + jnp.arange(per_block, dtype=jnp.int32)
    span_first = view_span[:, 0:1]
    span_length = view_span[:, 1:2]
    inside = (
        (brick_index[None, :] >= span_first) & (brick_index[None, :] < span_first + span_length)
    ).astype(jnp.float32)
    live_cells = jnp.repeat(inside, planes, axis=1)[:, :, None, None]
    counts = jnp.repeat(view_count.astype(jnp.float32), planes)[:, None, None]
    point_spread_kernels = psf_taps / jnp.sum(psf_taps, axis=-1, keepdims=True)
    fwd_x = banded_blur_matrix(point_spread_kernels[:, 0], block_x + 2 * reach, block_x, 0, 1)
    adj_x = banded_blur_matrix(
        point_spread_kernels[:, 0], block_x + 2 * reach, block_x, 2 * reach, -1
    )
    mat_y = banded_blur_matrix(point_spread_kernels[:, 1], ny_cells, ny_cells, reach, 1)
    mat_z = banded_blur_matrix(point_spread_kernels[:, 2], nz_cells, nz_cells, reach, 1)
    weights = view_weight[:, None, None, None]
    chunk_count = 4
    rows = ny_cells // chunk_count

    def forward_chunk(cells):
        padded = with_halo(cells, (("block", 0),), reach)
        along_x = jnp.einsum("wyz,vwx->vxyz", padded, fwd_x, precision=highest)
        return jnp.einsum("vxyz,vzq->vxyq", along_x, mat_z, precision=highest)

    def backward_chunk(back_y, cells, chunk):
        back_z = jnp.einsum("vxyz,vqz->vxyq", back_y, mat_z, precision=highest)
        rimmed = with_halo(back_z, (("block", 1),), reach)
        corrected = jnp.einsum("vwyz,vwx->vxyz", rimmed, adj_x, precision=highest)
        partial_logarithm = jnp.sum(live_cells * weights * jnp.log(corrected), axis=0)
        return view_sum_update(partial_logarithm, cells, counts)

    pieces = [
        lax.slice_in_dim(estimate, c * rows, (c + 1) * rows, axis=1) for c in range(chunk_count)
    ]
    forward = [forward_chunk(cells) for cells in pieces]
    for iteration in range(ITERS):
        along_xz = jnp.concatenate(forward, axis=2)
        blurred = jnp.einsum("vxyz,vyq->vxqz", along_xz, mat_y, precision=highest)
        ratios = live_cells * (obs_views / blurred) + (1.0 - live_cells)
        back_y = jnp.einsum("vxyz,vqy->vxqz", ratios, mat_y, precision=highest)
        updated = []
        forward = []
        for c in range(chunk_count):
            cells = backward_chunk(
                lax.slice_in_dim(back_y, c * rows, (c + 1) * rows, axis=2), pieces[c], c
            )
            updated.append(cells)
            if iteration + 1 < ITERS:
                forward.append(forward_chunk(cells))
        pieces = updated
    return jnp.concatenate(pieces, axis=1)


def solution(mesh):
    placed = (
        P("block", None, None),
        P("view", "block", None, None, None),
        P("view", "block"),
        P("view", "block"),
        P("view", None),
        P("block"),
        P("view", None, None),
        P("view"),
    )
    return jax.shard_map(
        on_device, mesh=mesh, in_specs=placed, out_specs=P("block", None, None), check_vma=False
    )
```

```python
import jax
import jax.numpy as jnp
from jax import lax
from jax.sharding import PartitionSpec as P

ITERS = 2


def with_halo(cells, sides, width):
    for axis, dim in sides:
        count = lax.axis_size(axis)
        ends = count - 1
        head = lax.slice_in_dim(cells, 0, width, axis=dim)
        tail = lax.slice_in_dim(cells, cells.shape[dim] - width, cells.shape[dim], axis=dim)
        cells = jnp.concatenate(
            [
                lax.ppermute(tail, axis, [(i, (i + 1) % count) for i in range(ends)]),
                cells,
                lax.ppermute(head, axis, [((i + 1) % count, i) for i in range(ends)]),
            ],
            axis=dim,
        )
    return cells


def view_sum_update(partial, current, counts):
    count = lax.axis_size("view")
    me = lax.axis_index("view")
    rows = partial.shape[0] // count
    quarters = partial.reshape((count, rows) + partial.shape[1:])
    arrived = lax.all_to_all(quarters, "view", split_axis=0, concat_axis=0, tiled=True)
    summed = jnp.sum(arrived, axis=0)
    own = lax.dynamic_slice_in_dim(current, me * rows, rows, axis=0)
    scale = lax.dynamic_slice_in_dim(counts, me * rows, rows, axis=0)
    updated = own * jnp.exp(summed / scale)
    copies = jnp.broadcast_to(updated[None], (count,) + updated.shape)
    gathered = lax.all_to_all(copies, "view", split_axis=0, concat_axis=0, tiled=True)
    return gathered.reshape(current.shape)


def banded_blur_matrix(filter_tap_values, row_count, col_count, offset_base, orientation):
    tap_count = filter_tap_values.shape[-1]
    grid_shape = (row_count, col_count, tap_count)
    row_index = lax.broadcasted_iota(jnp.int32, grid_shape, 0)
    col_index = lax.broadcasted_iota(jnp.int32, grid_shape, 1)
    tap_index = lax.broadcasted_iota(jnp.int32, grid_shape, 2)
    selected_entries = (orientation * (row_index - col_index) + offset_base == tap_index).astype(
        jnp.float32
    )
    return jnp.einsum(
        "ewq,gq->gew", selected_entries, filter_tap_values, precision=lax.Precision.HIGHEST
    )


def on_device(
    estimate, observed, route_dest, route_pos, view_span, view_count, psf_taps, view_weight
):
    highest = lax.Precision.HIGHEST
    blocks = lax.axis_size("block")
    slot_count = observed.shape[1]
    planes = observed.shape[2]
    ny_cells = observed.shape[3]
    nz_cells = observed.shape[4]
    per_group = view_span.shape[0]
    per_block = view_count.shape[0]
    capacity = max(1, slot_count // blocks)
    block_x = per_block * planes
    reach = psf_taps.shape[-1] // 2
    sources = observed[0]
    dest_list = route_dest[0]
    pos_list = route_pos[0]
    slot_index = jnp.arange(slot_count, dtype=jnp.int32)
    earlier = (dest_list[:, None] == dest_list[None, :]) & (
        slot_index[None, :] < slot_index[:, None]
    )
    rank_in_dest = jnp.sum(earlier.astype(jnp.int32), axis=1)
    target = jnp.where(dest_list >= 0, dest_list * capacity + rank_in_dest, blocks * capacity)
    outgoing = (
        jnp.zeros((blocks * capacity, planes, ny_cells, nz_cells), jnp.float32)
        .at[target]
        .set(sources, mode="drop")
    )
    out_pos = (
        jnp.full((blocks * capacity,), -1.0, jnp.float32)
        .at[target]
        .set(pos_list.astype(jnp.float32), mode="drop")
    )
    arrived, arrived_pos = (
        lax.all_to_all(
            outgoing.reshape(blocks, capacity, planes, ny_cells, nz_cells),
            "block",
            split_axis=0,
            concat_axis=0,
            tiled=True,
        ),
        lax.all_to_all(
            out_pos.reshape(blocks, capacity), "block", split_axis=0, concat_axis=0, tiled=True
        ),
    )
    places = arrived_pos.reshape(-1).astype(jnp.int32)
    places = jnp.where(places >= 0, places, per_group * per_block)
    placed = (
        jnp.zeros((per_group * per_block, planes, ny_cells, nz_cells), jnp.float32)
        .at[places]
        .set(arrived.reshape(-1, planes, ny_cells, nz_cells), mode="drop")
    )
    obs_views = placed.reshape(per_group, block_x, ny_cells, nz_cells)
    brick_index = lax.axis_index("block") * per_block + jnp.arange(per_block, dtype=jnp.int32)
    span_first = view_span[:, 0:1]
    span_length = view_span[:, 1:2]
    inside = (
        (brick_index[None, :] >= span_first) & (brick_index[None, :] < span_first + span_length)
    ).astype(jnp.float32)
    live_cells = jnp.repeat(inside, planes, axis=1)[:, :, None, None]
    counts = jnp.repeat(view_count.astype(jnp.float32), planes)[:, None, None]
    point_spread_kernels = psf_taps / jnp.sum(psf_taps, axis=-1, keepdims=True)
    fwd_x = banded_blur_matrix(point_spread_kernels[:, 0], block_x + 2 * reach, block_x, 0, 1)
    adj_x = banded_blur_matrix(
        point_spread_kernels[:, 0], block_x + 2 * reach, block_x, 2 * reach, -1
    )
    mat_y = banded_blur_matrix(point_spread_kernels[:, 1], ny_cells, ny_cells, reach, 1)
    mat_z = banded_blur_matrix(point_spread_kernels[:, 2], nz_cells, nz_cells, reach, 1)
    weights = view_weight[:, None, None, None]
    chunk_count = 4
    rows = ny_cells // chunk_count

    def forward_chunk(cells):
        padded = with_halo(cells, (("block", 0),), reach)
        along_x = jnp.einsum("wyz,vwx->vxyz", padded, fwd_x, precision=highest)
        return jnp.einsum("vxyz,vzq->vxyq", along_x, mat_z, precision=highest)

    def backward_chunk(back_y, cells, chunk):
        back_z = jnp.einsum("vxyz,vqz->vxyq", back_y, mat_z, precision=highest)
        rimmed = with_halo(back_z, (("block", 1),), reach)
        corrected = jnp.einsum("vwyz,vwx->vxyz", rimmed, adj_x, precision=highest)
        partial_logarithm = jnp.sum(live_cells * weights * jnp.log(corrected), axis=0)
        return view_sum_update(partial_logarithm, cells, counts)

    pieces = [
        lax.slice_in_dim(estimate, c * rows, (c + 1) * rows, axis=1) for c in range(chunk_count)
    ]
    forward = [forward_chunk(cells) for cells in pieces]
    for iteration in range(ITERS):
        along_xz = jnp.concatenate(forward, axis=2)
        blurred = jnp.einsum("vxyz,vyq->vxqz", along_xz, mat_y, precision=highest)
        ratios = live_cells * (obs_views / blurred) + (1.0 - live_cells)
        back_y = jnp.einsum("vxyz,vqy->vxqz", ratios, mat_y, precision=highest)
        updated = []
        forward = []
        for c in range(chunk_count):
            cells = backward_chunk(
                lax.slice_in_dim(back_y, c * rows, (c + 1) * rows, axis=2), pieces[c], c
            )
            updated.append(cells)
            if iteration + 1 < ITERS:
                forward.append(forward_chunk(cells))
        pieces = updated
    return jnp.concatenate(pieces, axis=1)


def solution(mesh):
    placed = (
        P("block", None, None),
        P("view", "block", None, None, None),
        P("view", "block"),
        P("view", "block"),
        P("view", None),
        P("block"),
        P("view", None, None),
        P("view"),
    )
    return jax.shard_map(
        on_device, mesh=mesh, in_specs=placed, out_specs=P("block", None, None), check_vma=False
    )
```

```python
import jax
import jax.numpy as jnp
from jax import lax
from jax.sharding import PartitionSpec as P

ITERS = 2


def with_halo(cells, sides, width):
    for axis, dim in sides:
        count = lax.axis_size(axis)
        ends = count - 1
        head = lax.slice_in_dim(cells, 0, width, axis=dim)
        tail = lax.slice_in_dim(cells, cells.shape[dim] - width, cells.shape[dim], axis=dim)
        cells = jnp.concatenate(
            [
                lax.ppermute(tail, axis, [(i, (i + 1) % count) for i in range(ends)]),
                cells,
                lax.ppermute(head, axis, [((i + 1) % count, i) for i in range(ends)]),
            ],
            axis=dim,
        )
    return cells


def view_sum_update(partial, current, counts):
    count = lax.axis_size("view")
    me = lax.axis_index("view")
    rows = partial.shape[0] // count

    def piece(cells, index):
        return lax.dynamic_slice_in_dim(cells, index * rows, rows, axis=0)

    summed = piece(partial, me)
    for shift in range(1, count):
        sent = piece(partial, (me + shift) % count)
        summed = summed + lax.ppermute(
            sent, "view", [(i, (i + shift) % count) for i in range(count)]
        )
    updated = piece(current, me) * jnp.exp(summed / piece(counts, me))
    gathered = lax.dynamic_update_slice_in_dim(current, updated, me * rows, axis=0)
    for shift in range(1, count):
        arrived = lax.ppermute(
            updated, "view", [(i, (i + shift) % count) for i in range(count)]
        )
        gathered = lax.dynamic_update_slice_in_dim(
            gathered, arrived, ((me - shift) % count) * rows, axis=0
        )
    return gathered


def banded_blur_matrix(filter_tap_values, row_count, col_count, offset_base, orientation):
    tap_count = filter_tap_values.shape[-1]
    grid_shape = (row_count, col_count, tap_count)
    row_index = lax.broadcasted_iota(jnp.int32, grid_shape, 0)
    col_index = lax.broadcasted_iota(jnp.int32, grid_shape, 1)
    tap_index = lax.broadcasted_iota(jnp.int32, grid_shape, 2)
    selected_entries = (orientation * (row_index - col_index) + offset_base == tap_index).astype(
        jnp.float32
    )
    return jnp.einsum(
        "ewq,gq->gew", selected_entries, filter_tap_values, precision=lax.Precision.HIGHEST
    )


def on_device(
    estimate, observed, route_dest, route_pos, view_span, view_count, psf_taps, view_weight
):
    highest = lax.Precision.HIGHEST
    blocks = lax.axis_size("block")
    slot_count = observed.shape[1]
    planes = observed.shape[2]
    ny_cells = observed.shape[3]
    nz_cells = observed.shape[4]
    per_group = view_span.shape[0]
    per_block = view_count.shape[0]
    capacity = max(1, slot_count // blocks)
    block_x = per_block * planes
    reach = psf_taps.shape[-1] // 2
    sources = observed[0]
    dest_list = route_dest[0]
    pos_list = route_pos[0]
    slot_index = jnp.arange(slot_count, dtype=jnp.int32)
    earlier = (dest_list[:, None] == dest_list[None, :]) & (
        slot_index[None, :] < slot_index[:, None]
    )
    rank_in_dest = jnp.sum(earlier.astype(jnp.int32), axis=1)
    target = jnp.where(dest_list >= 0, dest_list * capacity + rank_in_dest, blocks * capacity)
    outgoing = (
        jnp.zeros((blocks * capacity, planes, ny_cells, nz_cells), jnp.float32)
        .at[target]
        .set(sources, mode="drop")
    )
    out_pos = (
        jnp.full((blocks * capacity,), -1.0, jnp.float32)
        .at[target]
        .set(pos_list.astype(jnp.float32), mode="drop")
    )
    arrived, arrived_pos = (
        lax.all_to_all(
            outgoing.reshape(blocks, capacity, planes, ny_cells, nz_cells),
            "block",
            split_axis=0,
            concat_axis=0,
            tiled=True,
        ),
        lax.all_to_all(
            out_pos.reshape(blocks, capacity), "block", split_axis=0, concat_axis=0, tiled=True
        ),
    )
    places = arrived_pos.reshape(-1).astype(jnp.int32)
    places = jnp.where(places >= 0, places, per_group * per_block)
    placed = (
        jnp.zeros((per_group * per_block, planes, ny_cells, nz_cells), jnp.float32)
        .at[places]
        .set(arrived.reshape(-1, planes, ny_cells, nz_cells), mode="drop")
    )
    obs_views = placed.reshape(per_group, block_x, ny_cells, nz_cells)
    brick_index = lax.axis_index("block") * per_block + jnp.arange(per_block, dtype=jnp.int32)
    span_first = view_span[:, 0:1]
    span_length = view_span[:, 1:2]
    inside = (
        (brick_index[None, :] >= span_first) & (brick_index[None, :] < span_first + span_length)
    ).astype(jnp.float32)
    live_cells = jnp.repeat(inside, planes, axis=1)[:, :, None, None]
    counts = jnp.repeat(view_count.astype(jnp.float32), planes)[:, None, None]
    point_spread_kernels = psf_taps / jnp.sum(psf_taps, axis=-1, keepdims=True)
    fwd_x = banded_blur_matrix(point_spread_kernels[:, 0], block_x + 2 * reach, block_x, 0, 1)
    adj_x = banded_blur_matrix(
        point_spread_kernels[:, 0], block_x + 2 * reach, block_x, 2 * reach, -1
    )
    mat_y = banded_blur_matrix(point_spread_kernels[:, 1], ny_cells, ny_cells, reach, 1)
    mat_z = banded_blur_matrix(point_spread_kernels[:, 2], nz_cells, nz_cells, reach, 1)
    weights = view_weight[:, None, None, None]
    chunk_count = 2
    rows = ny_cells // chunk_count

    def forward_chunk(cells):
        padded = with_halo(cells, (("block", 0),), reach)
        along_x = jnp.einsum("wyz,vwx->vxyz", padded, fwd_x, precision=highest)
        return jnp.einsum("vxyz,vzq->vxyq", along_x, mat_z, precision=highest)

    def backward_chunk(back_y, cells, chunk):
        back_z = jnp.einsum("vxyz,vqz->vxyq", back_y, mat_z, precision=highest)
        rimmed = with_halo(back_z, (("block", 1),), reach)
        corrected = jnp.einsum("vwyz,vwx->vxyz", rimmed, adj_x, precision=highest)
        partial_logarithm = jnp.sum(live_cells * weights * jnp.log(corrected), axis=0)
        return view_sum_update(partial_logarithm, cells, counts)

    pieces = [
        lax.slice_in_dim(estimate, c * rows, (c + 1) * rows, axis=1) for c in range(chunk_count)
    ]
    forward = [forward_chunk(cells) for cells in pieces]
    for iteration in range(ITERS):
        along_xz = jnp.concatenate(forward, axis=2)
        blurred = jnp.einsum("vxyz,vyq->vxqz", along_xz, mat_y, precision=highest)
        ratios = live_cells * (obs_views / blurred) + (1.0 - live_cells)
        back_y = jnp.einsum("vxyz,vqy->vxqz", ratios, mat_y, precision=highest)
        updated = []
        forward = []
        for c in range(chunk_count):
            cells = backward_chunk(
                lax.slice_in_dim(back_y, c * rows, (c + 1) * rows, axis=2), pieces[c], c
            )
            updated.append(cells)
            if iteration + 1 < ITERS:
                forward.append(forward_chunk(cells))
        pieces = updated
    return jnp.concatenate(pieces, axis=1)


def solution(mesh):
    placed = (
        P("block", None, None),
        P("view", "block", None, None, None),
        P("view", "block"),
        P("view", "block"),
        P("view", None),
        P("block"),
        P("view", None, None),
        P("view"),
    )
    return jax.shard_map(
        on_device, mesh=mesh, in_specs=placed, out_specs=P("block", None, None), check_vma=False
    )
```

```python
import jax
import jax.numpy as jnp
from jax import lax
from jax.sharding import PartitionSpec as P

ITERS = 2


def with_halo(cells, sides, width):
    for axis, dim in sides:
        count = lax.axis_size(axis)
        ends = count - 1
        head = lax.slice_in_dim(cells, 0, width, axis=dim)
        tail = lax.slice_in_dim(cells, cells.shape[dim] - width, cells.shape[dim], axis=dim)
        cells = jnp.concatenate(
            [
                lax.ppermute(tail, axis, [(i, (i + 1) % count) for i in range(ends)]),
                cells,
                lax.ppermute(head, axis, [((i + 1) % count, i) for i in range(ends)]),
            ],
            axis=dim,
        )
    return cells


def view_sum_update(partial, current, counts):
    count = lax.axis_size("view")
    me = lax.axis_index("view")
    rows = partial.shape[0] // count

    def piece(cells, index):
        return lax.dynamic_slice_in_dim(cells, index * rows, rows, axis=0)

    summed = piece(partial, me)
    for shift in range(1, count):
        sent = piece(partial, (me + shift) % count)
        summed = summed + lax.ppermute(
            sent, "view", [(i, (i + shift) % count) for i in range(count)]
        )
    updated = piece(current, me) * jnp.exp(summed / piece(counts, me))
    gathered = lax.dynamic_update_slice_in_dim(current, updated, me * rows, axis=0)
    for shift in range(1, count):
        arrived = lax.ppermute(
            updated, "view", [(i, (i + shift) % count) for i in range(count)]
        )
        gathered = lax.dynamic_update_slice_in_dim(
            gathered, arrived, ((me - shift) % count) * rows, axis=0
        )
    return gathered


def banded_blur_matrix(filter_tap_values, row_count, col_count, offset_base, orientation):
    tap_count = filter_tap_values.shape[-1]
    grid_shape = (row_count, col_count, tap_count)
    row_index = lax.broadcasted_iota(jnp.int32, grid_shape, 0)
    col_index = lax.broadcasted_iota(jnp.int32, grid_shape, 1)
    tap_index = lax.broadcasted_iota(jnp.int32, grid_shape, 2)
    selected_entries = (orientation * (row_index - col_index) + offset_base == tap_index).astype(
        jnp.float32
    )
    return jnp.einsum(
        "ewq,gq->gew", selected_entries, filter_tap_values, precision=lax.Precision.HIGHEST
    )


def on_device(
    estimate, observed, route_dest, route_pos, view_span, view_count, psf_taps, view_weight
):
    highest = lax.Precision.HIGHEST
    blocks = lax.axis_size("block")
    slot_count = observed.shape[1]
    planes = observed.shape[2]
    ny_cells = observed.shape[3]
    nz_cells = observed.shape[4]
    per_group = view_span.shape[0]
    per_block = view_count.shape[0]
    block_x = per_block * planes
    reach = psf_taps.shape[-1] // 2
    sources = observed[0]
    dest_list = route_dest[0]
    pos_list = route_pos[0]
    block_ids = jnp.arange(blocks, dtype=jnp.int32)
    sends = dest_list[None, :] == block_ids[:, None]
    has_slot = jnp.any(sends, axis=1)
    slot_of = jnp.argmax(sends, axis=1)
    outgoing = jnp.where(
        has_slot[:, None, None, None], jnp.take(sources, slot_of, axis=0), 0.0
    )
    out_pos = jnp.where(has_slot, jnp.take(pos_list, slot_of).astype(jnp.float32), -1.0)
    arrived, arrived_pos = (
        lax.all_to_all(
            outgoing.reshape(blocks, 1, planes, ny_cells, nz_cells),
            "block",
            split_axis=0,
            concat_axis=0,
            tiled=True,
        ),
        lax.all_to_all(out_pos.reshape(blocks, 1), "block", split_axis=0, concat_axis=0, tiled=True),
    )
    arrived = arrived.reshape(blocks, planes, ny_cells, nz_cells)
    places = arrived_pos.reshape(-1).astype(jnp.int32)
    position_ids = jnp.arange(per_group * per_block, dtype=jnp.int32)
    holds = places[None, :] == position_ids[:, None]
    found = jnp.any(holds, axis=1)
    source_of = jnp.argmax(holds, axis=1)
    placed = jnp.where(found[:, None, None, None], jnp.take(arrived, source_of, axis=0), 0.0)
    obs_views = placed.reshape(per_group, block_x, ny_cells, nz_cells)
    brick_index = lax.axis_index("block") * per_block + jnp.arange(per_block, dtype=jnp.int32)
    span_first = view_span[:, 0:1]
    span_length = view_span[:, 1:2]
    inside = (
        (brick_index[None, :] >= span_first) & (brick_index[None, :] < span_first + span_length)
    ).astype(jnp.float32)
    live_cells = jnp.repeat(inside, planes, axis=1)[:, :, None, None]
    counts = jnp.repeat(view_count.astype(jnp.float32), planes)[:, None, None]
    point_spread_kernels = psf_taps / jnp.sum(psf_taps, axis=-1, keepdims=True)
    fwd_x = banded_blur_matrix(point_spread_kernels[:, 0], block_x + 2 * reach, block_x, 0, 1)
    adj_x = banded_blur_matrix(
        point_spread_kernels[:, 0], block_x + 2 * reach, block_x, 2 * reach, -1
    )
    mat_y = banded_blur_matrix(point_spread_kernels[:, 1], ny_cells, ny_cells, reach, 1)
    mat_z = banded_blur_matrix(point_spread_kernels[:, 2], nz_cells, nz_cells, reach, 1)
    weights = view_weight[:, None, None, None]
    chunk_count = 4
    rows = ny_cells // chunk_count

    def forward_chunk(cells):
        padded = with_halo(cells, (("block", 0),), reach)
        along_x = jnp.einsum("wyz,vwx->vxyz", padded, fwd_x, precision=highest)
        return jnp.einsum("vxyz,vzq->vxyq", along_x, mat_z, precision=highest)

    def backward_chunk(back_y, cells, chunk):
        back_z = jnp.einsum("vxyz,vqz->vxyq", back_y, mat_z, precision=highest)
        rimmed = with_halo(back_z, (("block", 1),), reach)
        corrected = jnp.einsum("vwyz,vwx->vxyz", rimmed, adj_x, precision=highest)
        partial_logarithm = jnp.sum(live_cells * weights * jnp.log(corrected), axis=0)
        return view_sum_update(partial_logarithm, cells, counts)

    pieces = [
        lax.slice_in_dim(estimate, c * rows, (c + 1) * rows, axis=1) for c in range(chunk_count)
    ]
    forward = [forward_chunk(cells) for cells in pieces]
    for iteration in range(ITERS):
        along_xz = jnp.concatenate(forward, axis=2)
        blurred = jnp.einsum("vxyz,vyq->vxqz", along_xz, mat_y, precision=highest)
        ratios = live_cells * (obs_views / blurred) + (1.0 - live_cells)
        back_y = jnp.einsum("vxyz,vqy->vxqz", ratios, mat_y, precision=highest)
        updated = []
        forward = []
        for c in range(chunk_count):
            cells = backward_chunk(
                lax.slice_in_dim(back_y, c * rows, (c + 1) * rows, axis=2), pieces[c], c
            )
            updated.append(cells)
            if iteration + 1 < ITERS:
                forward.append(forward_chunk(cells))
        pieces = updated
    return jnp.concatenate(pieces, axis=1)


def solution(mesh):
    placed = (
        P("block", None, None),
        P("view", "block", None, None, None),
        P("view", "block"),
        P("view", "block"),
        P("view", None),
        P("block"),
        P("view", None, None),
        P("view"),
    )
    return jax.shard_map(
        on_device, mesh=mesh, in_specs=placed, out_specs=P("block", None, None), check_vma=False
    )
```

```python
import jax
import jax.numpy as jnp
from jax import lax
from jax.sharding import PartitionSpec as P

ITERS = 2


def with_halo(cells, sides, width):
    for axis, dim in sides:
        count = lax.axis_size(axis)
        ends = count - 1
        head = lax.slice_in_dim(cells, 0, width, axis=dim)
        tail = lax.slice_in_dim(cells, cells.shape[dim] - width, cells.shape[dim], axis=dim)
        cells = jnp.concatenate(
            [
                lax.ppermute(tail, axis, [(i, (i + 1) % count) for i in range(ends)]),
                cells,
                lax.ppermute(head, axis, [((i + 1) % count, i) for i in range(ends)]),
            ],
            axis=dim,
        )
    return cells


def view_sum_update(partial, current, counts):
    count = lax.axis_size("view")
    me = lax.axis_index("view")
    rows = partial.shape[0] // count

    def piece(cells, index):
        return lax.dynamic_slice_in_dim(cells, index * rows, rows, axis=0)

    summed = piece(partial, me)
    for shift in range(1, count):
        sent = piece(partial, (me + shift) % count)
        summed = summed + lax.ppermute(
            sent, "view", [(i, (i + shift) % count) for i in range(count)]
        )
    updated = piece(current, me) * jnp.exp(summed / piece(counts, me))
    gathered = lax.dynamic_update_slice_in_dim(current, updated, me * rows, axis=0)
    for shift in range(1, count):
        arrived = lax.ppermute(
            updated, "view", [(i, (i + shift) % count) for i in range(count)]
        )
        gathered = lax.dynamic_update_slice_in_dim(
            gathered, arrived, ((me - shift) % count) * rows, axis=0
        )
    return gathered


def banded_blur_matrix(filter_tap_values, row_count, col_count, offset_base, orientation):
    tap_count = filter_tap_values.shape[-1]
    grid_shape = (row_count, col_count, tap_count)
    row_index = lax.broadcasted_iota(jnp.int32, grid_shape, 0)
    col_index = lax.broadcasted_iota(jnp.int32, grid_shape, 1)
    tap_index = lax.broadcasted_iota(jnp.int32, grid_shape, 2)
    selected_entries = (orientation * (row_index - col_index) + offset_base == tap_index).astype(
        jnp.float32
    )
    return jnp.einsum(
        "ewq,gq->gew", selected_entries, filter_tap_values, precision=lax.Precision.HIGHEST
    )


def on_device(
    estimate, observed, route_dest, route_pos, view_span, view_count, psf_taps, view_weight
):
    highest = lax.Precision.HIGHEST
    blocks = lax.axis_size("block")
    slot_count = observed.shape[1]
    planes = observed.shape[2]
    ny_cells = observed.shape[3]
    nz_cells = observed.shape[4]
    per_group = view_span.shape[0]
    per_block = view_count.shape[0]
    block_x = per_block * planes
    reach = psf_taps.shape[-1] // 2
    sources = observed[0]
    dest_list = route_dest[0]
    pos_list = route_pos[0]
    block_ids = jnp.arange(blocks, dtype=jnp.int32)
    sends = dest_list[None, :] == block_ids[:, None]
    slot_of = jnp.argmax(sends, axis=1)
    outgoing = jnp.take(sources, slot_of, axis=0)
    tables = lax.all_gather(jnp.stack([dest_list, pos_list]), "block")
    arrived = lax.all_to_all(
        outgoing.reshape(blocks, 1, planes, ny_cells, nz_cells),
        "block",
        split_axis=0,
        concat_axis=0,
        tiled=True,
    )
    arrived = arrived.reshape(blocks, planes, ny_cells, nz_cells)
    to_me = tables[:, 0, :] == lax.axis_index("block")
    places = jnp.where(
        jnp.any(to_me, axis=1),
        jnp.take_along_axis(tables[:, 1, :], jnp.argmax(to_me, axis=1)[:, None], axis=1)[:, 0],
        -1,
    )
    position_ids = jnp.arange(per_group * per_block, dtype=jnp.int32)
    holds = places[None, :] == position_ids[:, None]
    found = jnp.any(holds, axis=1)
    source_of = jnp.argmax(holds, axis=1)
    placed = jnp.where(found[:, None, None, None], jnp.take(arrived, source_of, axis=0), 0.0)
    obs_views = placed.reshape(per_group, block_x, ny_cells, nz_cells)
    brick_index = lax.axis_index("block") * per_block + jnp.arange(per_block, dtype=jnp.int32)
    span_first = view_span[:, 0:1]
    span_length = view_span[:, 1:2]
    inside = (
        (brick_index[None, :] >= span_first) & (brick_index[None, :] < span_first + span_length)
    ).astype(jnp.float32)
    live_cells = jnp.repeat(inside, planes, axis=1)[:, :, None, None]
    counts = jnp.repeat(view_count.astype(jnp.float32), planes)[:, None, None]
    point_spread_kernels = psf_taps / jnp.sum(psf_taps, axis=-1, keepdims=True)
    fwd_x = banded_blur_matrix(point_spread_kernels[:, 0], block_x + 2 * reach, block_x, 0, 1)
    adj_x = banded_blur_matrix(
        point_spread_kernels[:, 0], block_x + 2 * reach, block_x, 2 * reach, -1
    )
    mat_y = banded_blur_matrix(point_spread_kernels[:, 1], ny_cells, ny_cells, reach, 1)
    mat_z = banded_blur_matrix(point_spread_kernels[:, 2], nz_cells, nz_cells, reach, 1)
    weights = view_weight[:, None, None, None]
    chunk_count = 4
    rows = ny_cells // chunk_count

    def forward_chunk(cells):
        padded = with_halo(cells, (("block", 0),), reach)
        along_x = jnp.einsum("wyz,vwx->vxyz", padded, fwd_x, precision=highest)
        return jnp.einsum("vxyz,vzq->vxyq", along_x, mat_z, precision=highest)

    def backward_chunk(back_y, cells, chunk):
        back_z = jnp.einsum("vxyz,vqz->vxyq", back_y, mat_z, precision=highest)
        rimmed = with_halo(back_z, (("block", 1),), reach)
        corrected = jnp.einsum("vwyz,vwx->vxyz", rimmed, adj_x, precision=highest)
        partial_logarithm = jnp.sum(live_cells * weights * jnp.log(corrected), axis=0)
        return view_sum_update(partial_logarithm, cells, counts)

    pieces = [
        lax.slice_in_dim(estimate, c * rows, (c + 1) * rows, axis=1) for c in range(chunk_count)
    ]
    forward = [forward_chunk(cells) for cells in pieces]
    for iteration in range(ITERS):
        along_xz = jnp.concatenate(forward, axis=2)
        blurred = jnp.einsum("vxyz,vyq->vxqz", along_xz, mat_y, precision=highest)
        ratios = live_cells * (obs_views / blurred) + (1.0 - live_cells)
        back_y = jnp.einsum("vxyz,vqy->vxqz", ratios, mat_y, precision=highest)
        updated = []
        forward = []
        for c in range(chunk_count):
            cells = backward_chunk(
                lax.slice_in_dim(back_y, c * rows, (c + 1) * rows, axis=2), pieces[c], c
            )
            updated.append(cells)
            if iteration + 1 < ITERS:
                forward.append(forward_chunk(cells))
        pieces = updated
    return jnp.concatenate(pieces, axis=1)


def solution(mesh):
    placed = (
        P("block", None, None),
        P("view", "block", None, None, None),
        P("view", "block"),
        P("view", "block"),
        P("view", None),
        P("block"),
        P("view", None, None),
        P("view"),
    )
    return jax.shard_map(
        on_device, mesh=mesh, in_specs=placed, out_specs=P("block", None, None), check_vma=False
    )
```

```python
import jax
import jax.numpy as jnp
from jax import lax
from jax.sharding import PartitionSpec as P

ITERS = 2


def with_halo(cells, sides, width):
    for axis, dim in sides:
        count = lax.axis_size(axis)
        ends = count - 1
        head = lax.slice_in_dim(cells, 0, width, axis=dim)
        tail = lax.slice_in_dim(cells, cells.shape[dim] - width, cells.shape[dim], axis=dim)
        cells = jnp.concatenate(
            [
                lax.ppermute(tail, axis, [(i, (i + 1) % count) for i in range(ends)]),
                cells,
                lax.ppermute(head, axis, [((i + 1) % count, i) for i in range(ends)]),
            ],
            axis=dim,
        )
    return cells


def view_sum_update(partial, current, counts):
    count = lax.axis_size("view")
    me = lax.axis_index("view")
    rows = partial.shape[0] // count

    def piece(cells, index):
        return lax.dynamic_slice_in_dim(cells, index * rows, rows, axis=0)

    summed = piece(partial, me)
    for shift in range(1, count):
        sent = piece(partial, (me + shift) % count)
        summed = summed + lax.ppermute(
            sent, "view", [(i, (i + shift) % count) for i in range(count)]
        )
    updated = piece(current, me) * jnp.exp(summed / piece(counts, me))
    gathered = lax.dynamic_update_slice_in_dim(current, updated, me * rows, axis=0)
    for shift in range(1, count):
        arrived = lax.ppermute(
            updated, "view", [(i, (i + shift) % count) for i in range(count)]
        )
        gathered = lax.dynamic_update_slice_in_dim(
            gathered, arrived, ((me - shift) % count) * rows, axis=0
        )
    return gathered


def banded_blur_matrix(filter_tap_values, row_count, col_count, offset_base, orientation):
    tap_count = filter_tap_values.shape[-1]
    grid_shape = (row_count, col_count, tap_count)
    row_index = lax.broadcasted_iota(jnp.int32, grid_shape, 0)
    col_index = lax.broadcasted_iota(jnp.int32, grid_shape, 1)
    tap_index = lax.broadcasted_iota(jnp.int32, grid_shape, 2)
    selected_entries = (orientation * (row_index - col_index) + offset_base == tap_index).astype(
        jnp.float32
    )
    return jnp.einsum(
        "ewq,gq->gew", selected_entries, filter_tap_values, precision=lax.Precision.HIGHEST
    )


def on_device(
    estimate, observed, route_dest, route_pos, view_span, view_count, psf_taps, view_weight
):
    highest = lax.Precision.HIGHEST
    blocks = lax.axis_size("block")
    slot_count = observed.shape[1]
    planes = observed.shape[2]
    ny_cells = observed.shape[3]
    nz_cells = observed.shape[4]
    per_group = view_span.shape[0]
    per_block = view_count.shape[0]
    block_x = per_block * planes
    reach = psf_taps.shape[-1] // 2
    sources = observed[0]
    dest_list = route_dest[0]
    pos_list = route_pos[0]
    block_ids = jnp.arange(blocks, dtype=jnp.int32)
    sends = dest_list[None, :] == block_ids[:, None]
    has_slot = jnp.any(sends, axis=1)
    slot_of = jnp.argmax(sends, axis=1)
    outgoing = jnp.take(sources, slot_of, axis=0, mode="clip")
    out_pos = jnp.where(has_slot, jnp.take(pos_list, slot_of).astype(jnp.float32), -1.0)
    arrived, arrived_pos = (
        lax.all_to_all(
            outgoing.reshape(blocks, 1, planes, ny_cells, nz_cells),
            "block",
            split_axis=0,
            concat_axis=0,
            tiled=True,
        ),
        lax.all_to_all(out_pos.reshape(blocks, 1), "block", split_axis=0, concat_axis=0, tiled=True),
    )
    arrived = arrived.reshape(blocks, planes, ny_cells, nz_cells)
    places = arrived_pos.reshape(-1).astype(jnp.int32)
    position_ids = jnp.arange(per_group * per_block, dtype=jnp.int32)
    holds = places[None, :] == position_ids[:, None]
    found = jnp.any(holds, axis=1)
    source_of = jnp.argmax(holds, axis=1)
    placed = jnp.where(found[:, None, None, None], jnp.take(arrived, source_of, axis=0, mode="clip"), 0.0)
    obs_views = placed.reshape(per_group, block_x, ny_cells, nz_cells)
    brick_index = lax.axis_index("block") * per_block + jnp.arange(per_block, dtype=jnp.int32)
    span_first = view_span[:, 0:1]
    span_length = view_span[:, 1:2]
    inside = (
        (brick_index[None, :] >= span_first) & (brick_index[None, :] < span_first + span_length)
    ).astype(jnp.float32)
    live_cells = jnp.repeat(inside, planes, axis=1)[:, :, None, None]
    counts = jnp.repeat(view_count.astype(jnp.float32), planes)[:, None, None]
    point_spread_kernels = psf_taps / jnp.sum(psf_taps, axis=-1, keepdims=True)
    fwd_x = banded_blur_matrix(point_spread_kernels[:, 0], block_x + 2 * reach, block_x, 0, 1)
    adj_x = banded_blur_matrix(
        point_spread_kernels[:, 0], block_x + 2 * reach, block_x, 2 * reach, -1
    )
    mat_y = banded_blur_matrix(point_spread_kernels[:, 1], ny_cells, ny_cells, reach, 1)
    mat_z = banded_blur_matrix(point_spread_kernels[:, 2], nz_cells, nz_cells, reach, 1)
    weights = view_weight[:, None, None, None]
    chunk_count = 4
    rows = ny_cells // chunk_count

    def forward_chunk(cells):
        padded = with_halo(cells, (("block", 0),), reach)
        along_x = jnp.einsum("wyz,vwx->vxyz", padded, fwd_x, precision=highest)
        return jnp.einsum("vxyz,vzq->vxyq", along_x, mat_z, precision=highest)

    def backward_chunk(back_y, cells, chunk):
        back_z = jnp.einsum("vxyz,vqz->vxyq", back_y, mat_z, precision=highest)
        rimmed = with_halo(back_z, (("block", 1),), reach)
        corrected = jnp.einsum("vwyz,vwx->vxyz", rimmed, adj_x, precision=highest)
        partial_logarithm = jnp.sum(live_cells * weights * jnp.log(corrected), axis=0)
        return view_sum_update(partial_logarithm, cells, counts)

    pieces = [
        lax.slice_in_dim(estimate, c * rows, (c + 1) * rows, axis=1) for c in range(chunk_count)
    ]
    forward = [forward_chunk(cells) for cells in pieces]
    for iteration in range(ITERS):
        along_xz = jnp.concatenate(forward, axis=2)
        blurred = jnp.einsum("vxyz,vyq->vxqz", along_xz, mat_y, precision=highest)
        ratios = live_cells * (obs_views / blurred) + (1.0 - live_cells)
        back_y = jnp.einsum("vxyz,vqy->vxqz", ratios, mat_y, precision=highest)
        updated = []
        forward = []
        for c in range(chunk_count):
            cells = backward_chunk(
                lax.slice_in_dim(back_y, c * rows, (c + 1) * rows, axis=2), pieces[c], c
            )
            updated.append(cells)
            if iteration + 1 < ITERS:
                forward.append(forward_chunk(cells))
        pieces = updated
    return jnp.concatenate(pieces, axis=1)


def solution(mesh):
    placed = (
        P("block", None, None),
        P("view", "block", None, None, None),
        P("view", "block"),
        P("view", "block"),
        P("view", None),
        P("block"),
        P("view", None, None),
        P("view"),
    )
    return jax.shard_map(
        on_device, mesh=mesh, in_specs=placed, out_specs=P("block", None, None), check_vma=False
    )
```

```python
import jax
import jax.numpy as jnp
from jax import lax
from jax.sharding import PartitionSpec as P

ITERS = 2


def with_halo(cells, sides, width):
    for axis, dim in sides:
        count = lax.axis_size(axis)
        ends = count - 1
        head = lax.slice_in_dim(cells, 0, width, axis=dim)
        tail = lax.slice_in_dim(cells, cells.shape[dim] - width, cells.shape[dim], axis=dim)
        cells = jnp.concatenate(
            [
                lax.ppermute(tail, axis, [(i, (i + 1) % count) for i in range(ends)]),
                cells,
                lax.ppermute(head, axis, [((i + 1) % count, i) for i in range(ends)]),
            ],
            axis=dim,
        )
    return cells


def view_sum_update(partial, current, counts):
    me = lax.axis_index("view")
    low = me % 2
    high = me // 2
    rows = partial.shape[0] // 4
    tail = partial.shape[1:]
    near = [(i, i ^ 1) for i in range(4)]
    far = [(i, i ^ 2) for i in range(4)]
    split = partial.reshape((2, 2, rows) + tail)
    kept = lax.dynamic_index_in_dim(split, low, axis=1, keepdims=False)
    sent = lax.dynamic_index_in_dim(split, 1 - low, axis=1, keepdims=False)
    half = kept + lax.ppermute(sent, "view", near)
    kept = lax.dynamic_index_in_dim(half, high, axis=0, keepdims=False)
    sent = lax.dynamic_index_in_dim(half, 1 - high, axis=0, keepdims=False)
    summed = kept + lax.ppermute(sent, "view", far)
    own = lax.dynamic_slice_in_dim(current, me * rows, rows, axis=0)
    scale = lax.dynamic_slice_in_dim(counts, me * rows, rows, axis=0)
    updated = own * jnp.exp(summed / scale)
    other = lax.ppermute(updated, "view", far)
    pair = jnp.where(high == 0, jnp.stack([updated, other]), jnp.stack([other, updated]))
    other = lax.ppermute(pair, "view", near)
    whole = jnp.where(low == 0, jnp.stack([pair, other], axis=1), jnp.stack([other, pair], axis=1))
    return whole.reshape(current.shape)


def banded_blur_matrix(filter_tap_values, row_count, col_count, offset_base, orientation):
    tap_count = filter_tap_values.shape[-1]
    grid_shape = (row_count, col_count, tap_count)
    row_index = lax.broadcasted_iota(jnp.int32, grid_shape, 0)
    col_index = lax.broadcasted_iota(jnp.int32, grid_shape, 1)
    tap_index = lax.broadcasted_iota(jnp.int32, grid_shape, 2)
    selected_entries = (orientation * (row_index - col_index) + offset_base == tap_index).astype(
        jnp.float32
    )
    return jnp.einsum(
        "ewq,gq->gew", selected_entries, filter_tap_values, precision=lax.Precision.HIGHEST
    )


def on_device(
    estimate, observed, route_dest, route_pos, view_span, view_count, psf_taps, view_weight
):
    highest = lax.Precision.HIGHEST
    blocks = lax.axis_size("block")
    slot_count = observed.shape[1]
    planes = observed.shape[2]
    ny_cells = observed.shape[3]
    nz_cells = observed.shape[4]
    per_group = view_span.shape[0]
    per_block = view_count.shape[0]
    block_x = per_block * planes
    reach = psf_taps.shape[-1] // 2
    sources = observed[0]
    dest_list = route_dest[0]
    pos_list = route_pos[0]
    block_ids = jnp.arange(blocks, dtype=jnp.int32)
    sends = dest_list[None, :] == block_ids[:, None]
    has_slot = jnp.any(sends, axis=1)
    slot_of = jnp.argmax(sends, axis=1)
    outgoing = jnp.take(sources, slot_of, axis=0, mode="clip")
    out_pos = jnp.where(has_slot, jnp.take(pos_list, slot_of).astype(jnp.float32), -1.0)
    arrived, arrived_pos = (
        lax.all_to_all(
            outgoing.reshape(blocks, 1, planes, ny_cells, nz_cells),
            "block",
            split_axis=0,
            concat_axis=0,
            tiled=True,
        ),
        lax.all_to_all(out_pos.reshape(blocks, 1), "block", split_axis=0, concat_axis=0, tiled=True),
    )
    arrived = arrived.reshape(blocks, planes, ny_cells, nz_cells)
    places = arrived_pos.reshape(-1).astype(jnp.int32)
    position_ids = jnp.arange(per_group * per_block, dtype=jnp.int32)
    holds = places[None, :] == position_ids[:, None]
    found = jnp.any(holds, axis=1)
    source_of = jnp.argmax(holds, axis=1)
    placed = jnp.where(found[:, None, None, None], jnp.take(arrived, source_of, axis=0, mode="clip"), 0.0)
    obs_views = placed.reshape(per_group, block_x, ny_cells, nz_cells)
    brick_index = lax.axis_index("block") * per_block + jnp.arange(per_block, dtype=jnp.int32)
    span_first = view_span[:, 0:1]
    span_length = view_span[:, 1:2]
    inside = (
        (brick_index[None, :] >= span_first) & (brick_index[None, :] < span_first + span_length)
    ).astype(jnp.float32)
    live_cells = jnp.repeat(inside, planes, axis=1)[:, :, None, None]
    counts = jnp.repeat(view_count.astype(jnp.float32), planes)[:, None, None]
    point_spread_kernels = psf_taps / jnp.sum(psf_taps, axis=-1, keepdims=True)
    fwd_x = banded_blur_matrix(point_spread_kernels[:, 0], block_x + 2 * reach, block_x, 0, 1)
    adj_x = banded_blur_matrix(
        point_spread_kernels[:, 0], block_x + 2 * reach, block_x, 2 * reach, -1
    )
    mat_y = banded_blur_matrix(point_spread_kernels[:, 1], ny_cells, ny_cells, reach, 1)
    mat_z = banded_blur_matrix(point_spread_kernels[:, 2], nz_cells, nz_cells, reach, 1)
    weights = view_weight[:, None, None, None]
    chunk_count = 4
    rows = ny_cells // chunk_count

    def forward_chunk(cells):
        padded = with_halo(cells, (("block", 0),), reach)
        along_x = jnp.einsum("wyz,vwx->vxyz", padded, fwd_x, precision=highest)
        return jnp.einsum("vxyz,vzq->vxyq", along_x, mat_z, precision=highest)

    def backward_chunk(back_y, cells, chunk):
        back_z = jnp.einsum("vxyz,vqz->vxyq", back_y, mat_z, precision=highest)
        rimmed = with_halo(back_z, (("block", 1),), reach)
        corrected = jnp.einsum("vwyz,vwx->vxyz", rimmed, adj_x, precision=highest)
        partial_logarithm = jnp.sum(live_cells * weights * jnp.log(corrected), axis=0)
        return view_sum_update(partial_logarithm, cells, counts)

    pieces = [
        lax.slice_in_dim(estimate, c * rows, (c + 1) * rows, axis=1) for c in range(chunk_count)
    ]
    forward = [forward_chunk(cells) for cells in pieces]
    for iteration in range(ITERS):
        along_xz = jnp.concatenate(forward, axis=2)
        blurred = jnp.einsum("vxyz,vyq->vxqz", along_xz, mat_y, precision=highest)
        ratios = live_cells * (obs_views / blurred) + (1.0 - live_cells)
        back_y = jnp.einsum("vxyz,vqy->vxqz", ratios, mat_y, precision=highest)
        updated = []
        forward = []
        for c in range(chunk_count):
            cells = backward_chunk(
                lax.slice_in_dim(back_y, c * rows, (c + 1) * rows, axis=2), pieces[c], c
            )
            updated.append(cells)
            if iteration + 1 < ITERS:
                forward.append(forward_chunk(cells))
        pieces = updated
    return jnp.concatenate(pieces, axis=1)


def solution(mesh):
    placed = (
        P("block", None, None),
        P("view", "block", None, None, None),
        P("view", "block"),
        P("view", "block"),
        P("view", None),
        P("block"),
        P("view", None, None),
        P("view"),
    )
    return jax.shard_map(
        on_device, mesh=mesh, in_specs=placed, out_specs=P("block", None, None), check_vma=False
    )
```

```python
import jax
import jax.numpy as jnp
from jax import lax
from jax.sharding import PartitionSpec as P

ITERS = 2


def with_halo(cells, sides, width):
    for axis, dim in sides:
        count = lax.axis_size(axis)
        ends = count - 1
        head = lax.slice_in_dim(cells, 0, width, axis=dim)
        tail = lax.slice_in_dim(cells, cells.shape[dim] - width, cells.shape[dim], axis=dim)
        cells = jnp.concatenate(
            [
                lax.ppermute(tail, axis, [(i, (i + 1) % count) for i in range(ends)]),
                cells,
                lax.ppermute(head, axis, [((i + 1) % count, i) for i in range(ends)]),
            ],
            axis=dim,
        )
    return cells


def view_sum_update(partial, current, counts):
    count = lax.axis_size("view")
    me = lax.axis_index("view")
    rows = partial.shape[0] // count

    def piece(cells, index):
        return lax.dynamic_slice_in_dim(cells, index * rows, rows, axis=0)

    summed = piece(partial, me)
    for shift in range(1, count):
        sent = piece(partial, (me + shift) % count)
        summed = summed + lax.ppermute(
            sent, "view", [(i, (i + shift) % count) for i in range(count)]
        )
    updated = piece(current, me) * jnp.exp(summed / piece(counts, me))
    gathered = lax.dynamic_update_slice_in_dim(current, updated, me * rows, axis=0)
    for shift in range(1, count):
        arrived = lax.ppermute(
            updated, "view", [(i, (i + shift) % count) for i in range(count)]
        )
        gathered = lax.dynamic_update_slice_in_dim(
            gathered, arrived, ((me - shift) % count) * rows, axis=0
        )
    return gathered


def banded_blur_matrix(filter_tap_values, row_count, col_count, offset_base, orientation):
    tap_count = filter_tap_values.shape[-1]
    grid_shape = (row_count, col_count, tap_count)
    row_index = lax.broadcasted_iota(jnp.int32, grid_shape, 0)
    col_index = lax.broadcasted_iota(jnp.int32, grid_shape, 1)
    tap_index = lax.broadcasted_iota(jnp.int32, grid_shape, 2)
    selected_entries = (orientation * (row_index - col_index) + offset_base == tap_index).astype(
        jnp.float32
    )
    return jnp.einsum(
        "ewq,gq->gew", selected_entries, filter_tap_values, precision=lax.Precision.HIGHEST
    )


def on_device(
    estimate, observed, route_dest, route_pos, view_span, view_count, psf_taps, view_weight
):
    highest = lax.Precision.HIGHEST
    blocks = lax.axis_size("block")
    slot_count = observed.shape[1]
    planes = observed.shape[2]
    ny_cells = observed.shape[3]
    nz_cells = observed.shape[4]
    per_group = view_span.shape[0]
    per_block = view_count.shape[0]
    block_x = per_block * planes
    reach = psf_taps.shape[-1] // 2
    sources = observed[0]
    dest_list = route_dest[0]
    pos_list = route_pos[0]
    block_ids = jnp.arange(blocks, dtype=jnp.int32)
    sends = dest_list[None, :] == block_ids[:, None]
    has_slot = jnp.any(sends, axis=1)
    slot_of = jnp.argmax(sends, axis=1)
    outgoing = jnp.take(sources, slot_of, axis=0, mode="clip")
    rows = ny_cells // 4
    pieces = [lax.slice_in_dim(estimate, c * rows, (c + 1) * rows, axis=1) for c in range(4)]
    first = [with_halo(cells, (("block", 0),), reach) for cells in pieces]
    outgoing, first = lax.optimization_barrier((outgoing, first))
    out_pos = jnp.where(has_slot, jnp.take(pos_list, slot_of).astype(jnp.float32), -1.0)
    arrived, arrived_pos = (
        lax.all_to_all(
            outgoing.reshape(blocks, 1, planes, ny_cells, nz_cells),
            "block",
            split_axis=0,
            concat_axis=0,
            tiled=True,
        ),
        lax.all_to_all(out_pos.reshape(blocks, 1), "block", split_axis=0, concat_axis=0, tiled=True),
    )
    arrived = arrived.reshape(blocks, planes, ny_cells, nz_cells)
    places = arrived_pos.reshape(-1).astype(jnp.int32)
    position_ids = jnp.arange(per_group * per_block, dtype=jnp.int32)
    holds = places[None, :] == position_ids[:, None]
    found = jnp.any(holds, axis=1)
    source_of = jnp.argmax(holds, axis=1)
    placed = jnp.where(found[:, None, None, None], jnp.take(arrived, source_of, axis=0, mode="clip"), 0.0)
    obs_views = placed.reshape(per_group, block_x, ny_cells, nz_cells)
    brick_index = lax.axis_index("block") * per_block + jnp.arange(per_block, dtype=jnp.int32)
    span_first = view_span[:, 0:1]
    span_length = view_span[:, 1:2]
    inside = (
        (brick_index[None, :] >= span_first) & (brick_index[None, :] < span_first + span_length)
    ).astype(jnp.float32)
    live_cells = jnp.repeat(inside, planes, axis=1)[:, :, None, None]
    counts = jnp.repeat(view_count.astype(jnp.float32), planes)[:, None, None]
    point_spread_kernels = psf_taps / jnp.sum(psf_taps, axis=-1, keepdims=True)
    fwd_x = banded_blur_matrix(point_spread_kernels[:, 0], block_x + 2 * reach, block_x, 0, 1)
    adj_x = banded_blur_matrix(
        point_spread_kernels[:, 0], block_x + 2 * reach, block_x, 2 * reach, -1
    )
    mat_y = banded_blur_matrix(point_spread_kernels[:, 1], ny_cells, ny_cells, reach, 1)
    mat_z = banded_blur_matrix(point_spread_kernels[:, 2], nz_cells, nz_cells, reach, 1)
    weights = view_weight[:, None, None, None]
    chunk_count = len(pieces)

    def forward_chunk(cells):
        return forward_padded(with_halo(cells, (("block", 0),), reach))

    def forward_padded(padded):
        along_x = jnp.einsum("wyz,vwx->vxyz", padded, fwd_x, precision=highest)
        return jnp.einsum("vxyz,vzq->vxyq", along_x, mat_z, precision=highest)

    def backward_chunk(back_y, cells, chunk):
        back_z = jnp.einsum("vxyz,vqz->vxyq", back_y, mat_z, precision=highest)
        rimmed = with_halo(back_z, (("block", 1),), reach)
        corrected = jnp.einsum("vwyz,vwx->vxyz", rimmed, adj_x, precision=highest)
        partial_logarithm = jnp.sum(live_cells * weights * jnp.log(corrected), axis=0)
        return view_sum_update(partial_logarithm, cells, counts)

    forward = [forward_padded(padded) for padded in first]
    for iteration in range(ITERS):
        along_xz = jnp.concatenate(forward, axis=2)
        blurred = jnp.einsum("vxyz,vyq->vxqz", along_xz, mat_y, precision=highest)
        ratios = live_cells * (obs_views / blurred) + (1.0 - live_cells)
        back_y = jnp.einsum("vxyz,vqy->vxqz", ratios, mat_y, precision=highest)
        updated = []
        forward = []
        for c in range(chunk_count):
            cells = backward_chunk(
                lax.slice_in_dim(back_y, c * rows, (c + 1) * rows, axis=2), pieces[c], c
            )
            updated.append(cells)
            if iteration + 1 < ITERS:
                forward.append(forward_chunk(cells))
        pieces = updated
    return jnp.concatenate(pieces, axis=1)


def solution(mesh):
    placed = (
        P("block", None, None),
        P("view", "block", None, None, None),
        P("view", "block"),
        P("view", "block"),
        P("view", None),
        P("block"),
        P("view", None, None),
        P("view"),
    )
    return jax.shard_map(
        on_device, mesh=mesh, in_specs=placed, out_specs=P("block", None, None), check_vma=False
    )
```

```python
import jax
import jax.numpy as jnp
from jax import lax
from jax.sharding import PartitionSpec as P

ITERS = 2


def with_halo(cells, sides, width):
    for axis, dim in sides:
        count = lax.axis_size(axis)
        ends = count - 1
        head = lax.slice_in_dim(cells, 0, width, axis=dim)
        tail = lax.slice_in_dim(cells, cells.shape[dim] - width, cells.shape[dim], axis=dim)
        cells = jnp.concatenate(
            [
                lax.ppermute(tail, axis, [(i, (i + 1) % count) for i in range(ends)]),
                cells,
                lax.ppermute(head, axis, [((i + 1) % count, i) for i in range(ends)]),
            ],
            axis=dim,
        )
    return cells


def view_sum_update(partial, current, counts):
    count = lax.axis_size("view")
    me = lax.axis_index("view")
    rows = partial.shape[0] // count

    def piece(cells, index):
        return lax.dynamic_slice_in_dim(cells, index * rows, rows, axis=0)

    summed = piece(partial, me)
    for shift in range(1, count):
        sent = piece(partial, (me + shift) % count)
        summed = summed + lax.ppermute(
            sent, "view", [(i, (i + shift) % count) for i in range(count)]
        )
    updated = piece(current, me) * jnp.exp(summed / piece(counts, me))
    gathered = lax.dynamic_update_slice_in_dim(current, updated, me * rows, axis=0)
    for shift in range(1, count):
        arrived = lax.ppermute(
            updated, "view", [(i, (i + shift) % count) for i in range(count)]
        )
        gathered = lax.dynamic_update_slice_in_dim(
            gathered, arrived, ((me - shift) % count) * rows, axis=0
        )
    return gathered


def banded_blur_matrix(filter_tap_values, row_count, col_count, offset_base, orientation):
    tap_count = filter_tap_values.shape[-1]
    grid_shape = (row_count, col_count, tap_count)
    row_index = lax.broadcasted_iota(jnp.int32, grid_shape, 0)
    col_index = lax.broadcasted_iota(jnp.int32, grid_shape, 1)
    tap_index = lax.broadcasted_iota(jnp.int32, grid_shape, 2)
    selected_entries = (orientation * (row_index - col_index) + offset_base == tap_index).astype(
        jnp.float32
    )
    return jnp.einsum(
        "ewq,gq->gew", selected_entries, filter_tap_values, precision=lax.Precision.HIGHEST
    )


def on_device(
    estimate, observed, route_dest, route_pos, view_span, view_count, psf_taps, view_weight
):
    highest = lax.Precision.HIGH
    blocks = lax.axis_size("block")
    slot_count = observed.shape[1]
    planes = observed.shape[2]
    ny_cells = observed.shape[3]
    nz_cells = observed.shape[4]
    per_group = view_span.shape[0]
    per_block = view_count.shape[0]
    block_x = per_block * planes
    reach = psf_taps.shape[-1] // 2
    sources = observed[0]
    dest_list = route_dest[0]
    pos_list = route_pos[0]
    block_ids = jnp.arange(blocks, dtype=jnp.int32)
    sends = dest_list[None, :] == block_ids[:, None]
    has_slot = jnp.any(sends, axis=1)
    slot_of = jnp.argmax(sends, axis=1)
    outgoing = jnp.take(sources, slot_of, axis=0, mode="clip")
    out_pos = jnp.where(has_slot, jnp.take(pos_list, slot_of).astype(jnp.float32), -1.0)
    arrived, arrived_pos = (
        lax.all_to_all(
            outgoing.reshape(blocks, 1, planes, ny_cells, nz_cells),
            "block",
            split_axis=0,
            concat_axis=0,
            tiled=True,
        ),
        lax.all_to_all(out_pos.reshape(blocks, 1), "block", split_axis=0, concat_axis=0, tiled=True),
    )
    arrived = arrived.reshape(blocks, planes, ny_cells, nz_cells)
    places = arrived_pos.reshape(-1).astype(jnp.int32)
    position_ids = jnp.arange(per_group * per_block, dtype=jnp.int32)
    holds = places[None, :] == position_ids[:, None]
    found = jnp.any(holds, axis=1)
    source_of = jnp.argmax(holds, axis=1)
    placed = jnp.where(found[:, None, None, None], jnp.take(arrived, source_of, axis=0, mode="clip"), 0.0)
    obs_views = placed.reshape(per_group, block_x, ny_cells, nz_cells)
    brick_index = lax.axis_index("block") * per_block + jnp.arange(per_block, dtype=jnp.int32)
    span_first = view_span[:, 0:1]
    span_length = view_span[:, 1:2]
    inside = (
        (brick_index[None, :] >= span_first) & (brick_index[None, :] < span_first + span_length)
    ).astype(jnp.float32)
    live_cells = jnp.repeat(inside, planes, axis=1)[:, :, None, None]
    counts = jnp.repeat(view_count.astype(jnp.float32), planes)[:, None, None]
    point_spread_kernels = psf_taps / jnp.sum(psf_taps, axis=-1, keepdims=True)
    fwd_x = banded_blur_matrix(point_spread_kernels[:, 0], block_x + 2 * reach, block_x, 0, 1)
    adj_x = banded_blur_matrix(
        point_spread_kernels[:, 0], block_x + 2 * reach, block_x, 2 * reach, -1
    )
    mat_y = banded_blur_matrix(point_spread_kernels[:, 1], ny_cells, ny_cells, reach, 1)
    mat_z = banded_blur_matrix(point_spread_kernels[:, 2], nz_cells, nz_cells, reach, 1)
    weights = view_weight[:, None, None, None]
    chunk_count = 4
    rows = ny_cells // chunk_count

    def forward_chunk(cells):
        padded = with_halo(cells, (("block", 0),), reach)
        along_x = jnp.einsum("wyz,vwx->vxyz", padded, fwd_x, precision=highest)
        return jnp.einsum("vxyz,vzq->vxyq", along_x, mat_z, precision=highest)

    def backward_chunk(back_y, cells, chunk):
        back_z = jnp.einsum("vxyz,vqz->vxyq", back_y, mat_z, precision=highest)
        rimmed = with_halo(back_z, (("block", 1),), reach)
        corrected = jnp.einsum("vwyz,vwx->vxyz", rimmed, adj_x, precision=highest)
        partial_logarithm = jnp.sum(live_cells * weights * jnp.log(corrected), axis=0)
        return view_sum_update(partial_logarithm, cells, counts)

    pieces = [
        lax.slice_in_dim(estimate, c * rows, (c + 1) * rows, axis=1) for c in range(chunk_count)
    ]
    forward = [forward_chunk(cells) for cells in pieces]
    for iteration in range(ITERS):
        along_xz = jnp.concatenate(forward, axis=2)
        blurred = jnp.einsum("vxyz,vyq->vxqz", along_xz, mat_y, precision=highest)
        ratios = live_cells * (obs_views / blurred) + (1.0 - live_cells)
        back_y = jnp.einsum("vxyz,vqy->vxqz", ratios, mat_y, precision=highest)
        updated = []
        forward = []
        for c in range(chunk_count):
            cells = backward_chunk(
                lax.slice_in_dim(back_y, c * rows, (c + 1) * rows, axis=2), pieces[c], c
            )
            updated.append(cells)
            if iteration + 1 < ITERS:
                forward.append(forward_chunk(cells))
        pieces = updated
    return jnp.concatenate(pieces, axis=1)


def solution(mesh):
    placed = (
        P("block", None, None),
        P("view", "block", None, None, None),
        P("view", "block"),
        P("view", "block"),
        P("view", None),
        P("block"),
        P("view", None, None),
        P("view"),
    )
    return jax.shard_map(
        on_device, mesh=mesh, in_specs=placed, out_specs=P("block", None, None), check_vma=False
    )
```

```python
import jax
import jax.numpy as jnp
from jax import lax
from jax.sharding import PartitionSpec as P

ITERS = 2


def with_halo(cells, sides, width):
    for axis, dim in sides:
        count = lax.axis_size(axis)
        ends = count - 1
        head = lax.slice_in_dim(cells, 0, width, axis=dim)
        tail = lax.slice_in_dim(cells, cells.shape[dim] - width, cells.shape[dim], axis=dim)
        cells = jnp.concatenate(
            [
                lax.ppermute(tail, axis, [(i, (i + 1) % count) for i in range(ends)]),
                cells,
                lax.ppermute(head, axis, [((i + 1) % count, i) for i in range(ends)]),
            ],
            axis=dim,
        )
    return cells


def view_sum_update(partial, current, counts):
    count = lax.axis_size("view")
    me = lax.axis_index("view")
    rows = partial.shape[0] // count

    def piece(cells, index):
        return lax.dynamic_slice_in_dim(cells, index * rows, rows, axis=0)

    summed = piece(partial, me)
    for shift in range(1, count):
        sent = piece(partial, (me + shift) % count)
        summed = summed + lax.ppermute(
            sent, "view", [(i, (i + shift) % count) for i in range(count)]
        )
    updated = piece(current, me) * jnp.exp(summed / piece(counts, me))
    gathered = lax.dynamic_update_slice_in_dim(current, updated, me * rows, axis=0)
    for shift in range(1, count):
        arrived = lax.ppermute(
            updated, "view", [(i, (i + shift) % count) for i in range(count)]
        )
        gathered = lax.dynamic_update_slice_in_dim(
            gathered, arrived, ((me - shift) % count) * rows, axis=0
        )
    return gathered


def banded_blur_matrix(filter_tap_values, row_count, col_count, offset_base, orientation):
    tap_count = filter_tap_values.shape[-1]
    grid_shape = (row_count, col_count, tap_count)
    row_index = lax.broadcasted_iota(jnp.int32, grid_shape, 0)
    col_index = lax.broadcasted_iota(jnp.int32, grid_shape, 1)
    tap_index = lax.broadcasted_iota(jnp.int32, grid_shape, 2)
    selected_entries = (orientation * (row_index - col_index) + offset_base == tap_index).astype(
        jnp.float32
    )
    return jnp.einsum(
        "ewq,gq->gew", selected_entries, filter_tap_values, precision=lax.Precision.HIGHEST
    )


def on_device(
    estimate, observed, route_dest, route_pos, view_span, view_count, psf_taps, view_weight
):
    highest = lax.Precision.HIGH
    blocks = lax.axis_size("block")
    slot_count = observed.shape[1]
    planes = observed.shape[2]
    ny_cells = observed.shape[3]
    nz_cells = observed.shape[4]
    per_group = view_span.shape[0]
    per_block = view_count.shape[0]
    block_x = per_block * planes
    reach = psf_taps.shape[-1] // 2
    sources = observed[0]
    dest_list = route_dest[0]
    pos_list = route_pos[0]
    block_ids = jnp.arange(blocks, dtype=jnp.int32)
    sends = dest_list[None, :] == block_ids[:, None]
    has_slot = jnp.any(sends, axis=1)
    slot_of = jnp.argmax(sends, axis=1)
    outgoing = jnp.take(sources, slot_of, axis=0, mode="clip")
    out_pos = jnp.where(has_slot, jnp.take(pos_list, slot_of).astype(jnp.float32), -1.0)
    arrived, arrived_pos = (
        lax.all_to_all(
            outgoing.reshape(blocks, 1, planes, ny_cells, nz_cells),
            "block",
            split_axis=0,
            concat_axis=0,
            tiled=True,
        ),
        lax.all_to_all(out_pos.reshape(blocks, 1), "block", split_axis=0, concat_axis=0, tiled=True),
    )
    arrived = arrived.reshape(blocks, planes, ny_cells, nz_cells)
    places = arrived_pos.reshape(-1).astype(jnp.int32)
    position_ids = jnp.arange(per_group * per_block, dtype=jnp.int32)
    holds = places[None, :] == position_ids[:, None]
    found = jnp.any(holds, axis=1)
    source_of = jnp.argmax(holds, axis=1)
    placed = jnp.where(found[:, None, None, None], jnp.take(arrived, source_of, axis=0, mode="clip"), 0.0)
    obs_views = placed.reshape(per_group, block_x, ny_cells, nz_cells)
    brick_index = lax.axis_index("block") * per_block + jnp.arange(per_block, dtype=jnp.int32)
    span_first = view_span[:, 0:1]
    span_length = view_span[:, 1:2]
    inside = (
        (brick_index[None, :] >= span_first) & (brick_index[None, :] < span_first + span_length)
    ).astype(jnp.float32)
    live_cells = jnp.repeat(inside, planes, axis=1)[:, :, None, None]
    counts = jnp.repeat(view_count.astype(jnp.float32), planes)[:, None, None]
    point_spread_kernels = psf_taps / jnp.sum(psf_taps, axis=-1, keepdims=True)
    fwd_x = banded_blur_matrix(point_spread_kernels[:, 0], block_x + 2 * reach, block_x, 0, 1)
    adj_x = banded_blur_matrix(
        point_spread_kernels[:, 0], block_x + 2 * reach, block_x, 2 * reach, -1
    )
    mat_y = banded_blur_matrix(point_spread_kernels[:, 1], ny_cells, ny_cells, reach, 1)
    mat_z = banded_blur_matrix(point_spread_kernels[:, 2], nz_cells, nz_cells, reach, 1)
    weights = view_weight[:, None, None, None]
    chunk_count = 4
    rows = ny_cells // chunk_count

    def forward_chunk(cells):
        padded = with_halo(cells, (("block", 0),), reach)
        along_x = jnp.einsum("wyz,vwx->vxyz", padded, fwd_x, precision=highest)
        return jnp.einsum("vxyz,vzq->vxyq", along_x, mat_z, precision=highest)

    def backward_chunk(back_y):
        back_z = jnp.einsum("vxyz,vqz->vxyq", back_y, mat_z, precision=highest)
        rimmed = with_halo(back_z, (("block", 1),), reach)
        corrected = jnp.einsum("vwyz,vwx->vxyz", rimmed, adj_x, precision=highest)
        return jnp.sum(live_cells * weights * jnp.log(corrected), axis=0)

    pieces = [
        lax.slice_in_dim(estimate, c * rows, (c + 1) * rows, axis=1) for c in range(chunk_count)
    ]
    forward = [forward_chunk(cells) for cells in pieces]
    for iteration in range(ITERS):
        along_xz = jnp.concatenate(forward, axis=2)
        blurred = jnp.einsum("vxyz,vyq->vxqz", along_xz, mat_y, precision=highest)
        ratios = live_cells * (obs_views / blurred) + (1.0 - live_cells)
        back_y = jnp.einsum("vxyz,vqy->vxqz", ratios, mat_y, precision=highest)
        updated = []
        forward = []
        for c in range(0, chunk_count, 2):
            logs = [
                backward_chunk(lax.slice_in_dim(back_y, k * rows, (k + 1) * rows, axis=2))
                for k in (c, c + 1)
            ]
            joined = view_sum_update(
                jnp.concatenate(logs, axis=1),
                jnp.concatenate(pieces[c : c + 2], axis=1),
                counts,
            )
            for k in range(2):
                cells = lax.slice_in_dim(joined, k * rows, (k + 1) * rows, axis=1)
                updated.append(cells)
                if iteration + 1 < ITERS:
                    forward.append(forward_chunk(cells))
        pieces = updated
    return jnp.concatenate(pieces, axis=1)


def solution(mesh):
    placed = (
        P("block", None, None),
        P("view", "block", None, None, None),
        P("view", "block"),
        P("view", "block"),
        P("view", None),
        P("block"),
        P("view", None, None),
        P("view"),
    )
    return jax.shard_map(
        on_device, mesh=mesh, in_specs=placed, out_specs=P("block", None, None), check_vma=False
    )
```

```python
import jax
import jax.numpy as jnp
from jax import lax
from jax.sharding import PartitionSpec as P

ITERS = 2


def with_halo(cells, sides, width):
    for axis, dim in sides:
        count = lax.axis_size(axis)
        ends = count - 1
        head = lax.slice_in_dim(cells, 0, width, axis=dim)
        tail = lax.slice_in_dim(cells, cells.shape[dim] - width, cells.shape[dim], axis=dim)
        cells = jnp.concatenate(
            [
                lax.ppermute(tail, axis, [(i, (i + 1) % count) for i in range(ends)]),
                cells,
                lax.ppermute(head, axis, [((i + 1) % count, i) for i in range(ends)]),
            ],
            axis=dim,
        )
    return cells


def view_sum_update(partial, current, counts):
    count = lax.axis_size("view")
    me = lax.axis_index("view")
    rows = partial.shape[0] // count

    def piece(cells, index):
        return lax.dynamic_slice_in_dim(cells, index * rows, rows, axis=0)

    summed = piece(partial, me)
    for shift in range(1, count):
        sent = piece(partial, (me + shift) % count)
        summed = summed + lax.ppermute(
            sent, "view", [(i, (i + shift) % count) for i in range(count)]
        )
    updated = piece(current, me) * jnp.exp(summed / piece(counts, me))
    gathered = lax.dynamic_update_slice_in_dim(current, updated, me * rows, axis=0)
    for shift in range(1, count):
        arrived = lax.ppermute(
            updated, "view", [(i, (i + shift) % count) for i in range(count)]
        )
        gathered = lax.dynamic_update_slice_in_dim(
            gathered, arrived, ((me - shift) % count) * rows, axis=0
        )
    return gathered


def banded_blur_matrix(filter_tap_values, row_count, col_count, offset_base, orientation):
    tap_count = filter_tap_values.shape[-1]
    grid_shape = (row_count, col_count, tap_count)
    row_index = lax.broadcasted_iota(jnp.int32, grid_shape, 0)
    col_index = lax.broadcasted_iota(jnp.int32, grid_shape, 1)
    tap_index = lax.broadcasted_iota(jnp.int32, grid_shape, 2)
    selected_entries = (orientation * (row_index - col_index) + offset_base == tap_index).astype(
        jnp.float32
    )
    return jnp.einsum(
        "ewq,gq->gew", selected_entries, filter_tap_values, precision=lax.Precision.HIGHEST
    )


def on_device(
    estimate, observed, route_dest, route_pos, view_span, view_count, psf_taps, view_weight
):
    highest = lax.Precision.HIGH
    blocks = lax.axis_size("block")
    slot_count = observed.shape[1]
    planes = observed.shape[2]
    ny_cells = observed.shape[3]
    nz_cells = observed.shape[4]
    per_group = view_span.shape[0]
    per_block = view_count.shape[0]
    block_x = per_block * planes
    reach = psf_taps.shape[-1] // 2
    sources = observed[0]
    dest_list = route_dest[0]
    pos_list = route_pos[0]
    block_ids = jnp.arange(blocks, dtype=jnp.int32)
    sends = dest_list[None, :] == block_ids[:, None]
    has_slot = jnp.any(sends, axis=1)
    slot_of = jnp.argmax(sends, axis=1)
    outgoing = jnp.take(sources, slot_of, axis=0, mode="clip")
    out_pos = jnp.where(has_slot, jnp.take(pos_list, slot_of).astype(jnp.float32), -1.0)
    arrived, arrived_pos = (
        lax.all_to_all(
            outgoing.reshape(blocks, 1, planes, ny_cells, nz_cells),
            "block",
            split_axis=0,
            concat_axis=0,
            tiled=True,
        ),
        lax.all_to_all(out_pos.reshape(blocks, 1), "block", split_axis=0, concat_axis=0, tiled=True),
    )
    arrived = arrived.reshape(blocks, planes, ny_cells, nz_cells)
    places = arrived_pos.reshape(-1).astype(jnp.int32)
    position_ids = jnp.arange(per_group * per_block, dtype=jnp.int32)
    holds = places[None, :] == position_ids[:, None]
    found = jnp.any(holds, axis=1)
    source_of = jnp.argmax(holds, axis=1)
    placed = jnp.where(found[:, None, None, None], jnp.take(arrived, source_of, axis=0, mode="clip"), 0.0)
    obs_views = placed.reshape(per_group, block_x, ny_cells, nz_cells)
    brick_index = lax.axis_index("block") * per_block + jnp.arange(per_block, dtype=jnp.int32)
    span_first = view_span[:, 0:1]
    span_length = view_span[:, 1:2]
    inside = (
        (brick_index[None, :] >= span_first) & (brick_index[None, :] < span_first + span_length)
    ).astype(jnp.float32)
    live_cells = jnp.repeat(inside, planes, axis=1)[:, :, None, None]
    counts = jnp.repeat(view_count.astype(jnp.float32), planes)[:, None, None]
    point_spread_kernels = psf_taps / jnp.sum(psf_taps, axis=-1, keepdims=True)
    fwd_x = banded_blur_matrix(point_spread_kernels[:, 0], block_x + 2 * reach, block_x, 0, 1)
    adj_x = banded_blur_matrix(
        point_spread_kernels[:, 0], block_x + 2 * reach, block_x, 2 * reach, -1
    )
    mat_y = banded_blur_matrix(point_spread_kernels[:, 1], ny_cells, ny_cells, reach, 1)
    mat_z = banded_blur_matrix(point_spread_kernels[:, 2], nz_cells, nz_cells, reach, 1)
    weights = view_weight[:, None, None, None]
    chunk_count = 8
    rows = ny_cells // chunk_count

    def forward_chunk(cells):
        padded = with_halo(cells, (("block", 0),), reach)
        along_x = jnp.einsum("wyz,vwx->vxyz", padded, fwd_x, precision=highest)
        return jnp.einsum("vxyz,vzq->vxyq", along_x, mat_z, precision=highest)

    def backward_chunk(back_y, cells, chunk):
        back_z = jnp.einsum("vxyz,vqz->vxyq", back_y, mat_z, precision=highest)
        rimmed = with_halo(back_z, (("block", 1),), reach)
        corrected = jnp.einsum("vwyz,vwx->vxyz", rimmed, adj_x, precision=highest)
        partial_logarithm = jnp.sum(live_cells * weights * jnp.log(corrected), axis=0)
        return view_sum_update(partial_logarithm, cells, counts)

    pieces = [
        lax.slice_in_dim(estimate, c * rows, (c + 1) * rows, axis=1) for c in range(chunk_count)
    ]
    forward = [forward_chunk(cells) for cells in pieces]
    for iteration in range(ITERS):
        along_xz = jnp.concatenate(forward, axis=2)
        blurred = jnp.einsum("vxyz,vyq->vxqz", along_xz, mat_y, precision=highest)
        ratios = live_cells * (obs_views / blurred) + (1.0 - live_cells)
        back_y = jnp.einsum("vxyz,vqy->vxqz", ratios, mat_y, precision=highest)
        updated = []
        forward = []
        for c in range(chunk_count):
            cells = backward_chunk(
                lax.slice_in_dim(back_y, c * rows, (c + 1) * rows, axis=2), pieces[c], c
            )
            updated.append(cells)
            if iteration + 1 < ITERS:
                forward.append(forward_chunk(cells))
        pieces = updated
    return jnp.concatenate(pieces, axis=1)


def solution(mesh):
    placed = (
        P("block", None, None),
        P("view", "block", None, None, None),
        P("view", "block"),
        P("view", "block"),
        P("view", None),
        P("block"),
        P("view", None, None),
        P("view"),
    )
    return jax.shard_map(
        on_device, mesh=mesh, in_specs=placed, out_specs=P("block", None, None), check_vma=False
    )
```

```python
import jax
import jax.numpy as jnp
from jax import lax
from jax.sharding import PartitionSpec as P

ITERS = 2


def with_halo(cells, sides, width):
    for axis, dim in sides:
        count = lax.axis_size(axis)
        ends = count - 1
        head = lax.slice_in_dim(cells, 0, width, axis=dim)
        tail = lax.slice_in_dim(cells, cells.shape[dim] - width, cells.shape[dim], axis=dim)
        cells = jnp.concatenate(
            [
                lax.ppermute(tail, axis, [(i, (i + 1) % count) for i in range(ends)]),
                cells,
                lax.ppermute(head, axis, [((i + 1) % count, i) for i in range(ends)]),
            ],
            axis=dim,
        )
    return cells


def view_sum_update(partial, current, counts):
    count = lax.axis_size("view")
    me = lax.axis_index("view")
    rows = partial.shape[0] // count

    def piece(cells, index):
        return lax.dynamic_slice_in_dim(cells, index * rows, rows, axis=0)

    summed = piece(partial, me)
    for shift in range(1, count):
        sent = piece(partial, (me + shift) % count)
        summed = summed + lax.ppermute(
            sent, "view", [(i, (i + shift) % count) for i in range(count)]
        )
    updated = piece(current, me) * jnp.exp(summed / piece(counts, me))
    gathered = lax.dynamic_update_slice_in_dim(current, updated, me * rows, axis=0)
    for shift in range(1, count):
        arrived = lax.ppermute(
            updated, "view", [(i, (i + shift) % count) for i in range(count)]
        )
        gathered = lax.dynamic_update_slice_in_dim(
            gathered, arrived, ((me - shift) % count) * rows, axis=0
        )
    return gathered


def banded_blur_matrix(filter_tap_values, row_count, col_count, offset_base, orientation):
    tap_count = filter_tap_values.shape[-1]
    grid_shape = (row_count, col_count, tap_count)
    row_index = lax.broadcasted_iota(jnp.int32, grid_shape, 0)
    col_index = lax.broadcasted_iota(jnp.int32, grid_shape, 1)
    tap_index = lax.broadcasted_iota(jnp.int32, grid_shape, 2)
    selected_entries = (orientation * (row_index - col_index) + offset_base == tap_index).astype(
        jnp.float32
    )
    return jnp.einsum(
        "ewq,gq->gew", selected_entries, filter_tap_values, precision=lax.Precision.HIGHEST
    )


def on_device(
    estimate, observed, route_dest, route_pos, view_span, view_count, psf_taps, view_weight
):
    highest = lax.Precision.HIGH
    blocks = lax.axis_size("block")
    slot_count = observed.shape[1]
    planes = observed.shape[2]
    ny_cells = observed.shape[3]
    nz_cells = observed.shape[4]
    per_group = view_span.shape[0]
    per_block = view_count.shape[0]
    block_x = per_block * planes
    reach = psf_taps.shape[-1] // 2
    sources = observed[0]
    dest_list = route_dest[0]
    pos_list = route_pos[0]
    block_ids = jnp.arange(blocks, dtype=jnp.int32)
    sends = dest_list[None, :] == block_ids[:, None]
    has_slot = jnp.any(sends, axis=1)
    slot_of = jnp.argmax(sends, axis=1)
    outgoing = jnp.take(sources, slot_of, axis=0, mode="clip")
    out_pos = jnp.where(has_slot, jnp.take(pos_list, slot_of).astype(jnp.float32), -1.0)
    arrived, arrived_pos = (
        lax.all_to_all(
            outgoing.reshape(blocks, 1, planes, ny_cells, nz_cells),
            "block",
            split_axis=0,
            concat_axis=0,
            tiled=True,
        ),
        lax.all_to_all(out_pos.reshape(blocks, 1), "block", split_axis=0, concat_axis=0, tiled=True),
    )
    arrived = arrived.reshape(blocks, planes, ny_cells, nz_cells)
    places = arrived_pos.reshape(-1).astype(jnp.int32)
    position_ids = jnp.arange(per_group * per_block, dtype=jnp.int32)
    holds = places[None, :] == position_ids[:, None]
    found = jnp.any(holds, axis=1)
    source_of = jnp.argmax(holds, axis=1)
    placed = jnp.where(found[:, None, None, None], jnp.take(arrived, source_of, axis=0, mode="clip"), 0.0)
    obs_views = placed.reshape(per_group, block_x, ny_cells, nz_cells)
    brick_index = lax.axis_index("block") * per_block + jnp.arange(per_block, dtype=jnp.int32)
    span_first = view_span[:, 0:1]
    span_length = view_span[:, 1:2]
    inside = (
        (brick_index[None, :] >= span_first) & (brick_index[None, :] < span_first + span_length)
    ).astype(jnp.float32)
    live_cells = jnp.repeat(inside, planes, axis=1)[:, :, None, None]
    counts = jnp.repeat(view_count.astype(jnp.float32), planes)[:, None, None]
    point_spread_kernels = psf_taps / jnp.sum(psf_taps, axis=-1, keepdims=True)
    fwd_x = banded_blur_matrix(point_spread_kernels[:, 0], block_x + 2 * reach, block_x, 0, 1)
    adj_x = banded_blur_matrix(
        point_spread_kernels[:, 0], block_x + 2 * reach, block_x, 2 * reach, -1
    )
    mat_y = banded_blur_matrix(point_spread_kernels[:, 1], ny_cells, ny_cells, reach, 1)
    mat_z = banded_blur_matrix(point_spread_kernels[:, 2], nz_cells, nz_cells, reach, 1)
    weights = view_weight[:, None, None, None]
    chunk_count = 2
    rows = ny_cells // chunk_count

    def forward_chunk(cells):
        padded = with_halo(cells, (("block", 0),), reach)
        along_x = jnp.einsum("wyz,vwx->vxyz", padded, fwd_x, precision=highest)
        return jnp.einsum("vxyz,vzq->vxyq", along_x, mat_z, precision=highest)

    def backward_chunk(back_y, cells, chunk):
        back_z = jnp.einsum("vxyz,vqz->vxyq", back_y, mat_z, precision=highest)
        rimmed = with_halo(back_z, (("block", 1),), reach)
        corrected = jnp.einsum("vwyz,vwx->vxyz", rimmed, adj_x, precision=highest)
        partial_logarithm = jnp.sum(live_cells * weights * jnp.log(corrected), axis=0)
        return view_sum_update(partial_logarithm, cells, counts)

    pieces = [
        lax.slice_in_dim(estimate, c * rows, (c + 1) * rows, axis=1) for c in range(chunk_count)
    ]
    forward = [forward_chunk(cells) for cells in pieces]
    for iteration in range(ITERS):
        along_xz = jnp.concatenate(forward, axis=2)
        blurred = jnp.einsum("vxyz,vyq->vxqz", along_xz, mat_y, precision=highest)
        ratios = live_cells * (obs_views / blurred) + (1.0 - live_cells)
        back_y = jnp.einsum("vxyz,vqy->vxqz", ratios, mat_y, precision=highest)
        updated = []
        forward = []
        for c in range(chunk_count):
            cells = backward_chunk(
                lax.slice_in_dim(back_y, c * rows, (c + 1) * rows, axis=2), pieces[c], c
            )
            updated.append(cells)
            if iteration + 1 < ITERS:
                forward.append(forward_chunk(cells))
        pieces = updated
    return jnp.concatenate(pieces, axis=1)


def solution(mesh):
    placed = (
        P("block", None, None),
        P("view", "block", None, None, None),
        P("view", "block"),
        P("view", "block"),
        P("view", None),
        P("block"),
        P("view", None, None),
        P("view"),
    )
    return jax.shard_map(
        on_device, mesh=mesh, in_specs=placed, out_specs=P("block", None, None), check_vma=False
    )
```
